256 devices in a mesh: lat: 8 (over x_lo, y), lon: 32 (over z, x_hi, core).
Axes of the slice: x: 4 (x_hi: 2, x_lo: 2; x = x_hi * 2 + x_lo), y: 4, z: 8, core: 2. Of those that a mesh axis runs over, the one named last changes fastest.
Arguments:
- features: bfloat16 [768, 1024, 256], P('lat', 'lon'), may hold values from -6 to 6
- quad_weights: float32 [768, 3, 129], P('lat'), may hold values from -6 to 6
- cycle_index: int32 [768, 3, 129], P('lat'), may hold values from 0 to 8
- widths: int32 [768], P('lat'), may hold values from 1 to 64, as said below
- mix_weight: bfloat16 [9, 256, 256], replicated, may hold values from -0.125 to 0.125
Outputs:
- mixed: bfloat16 [768, 1024, 256], P('lat', 'lon')
The draws below stay inside these ranges and needn't reach their ends.
Inputs may be any that keep to these rules, and one draw needn't show every extreme that they name: Rows within 8 rows of either end of the grid have widths above 32; rows 0 and 767 have exactly 64. All other rows have widths of at most 16, which row 8 reaches.
All inputs are finite; a program needn't handle non-finite values.
Results may differ from the reference program's by a relative error of at most 0.0031.
Values may be sent and summed in bfloat16 or wider, within the bound.
No kernel may reach another device: no remote copies, remote signals or barrier semaphores. Data moves between devices by JAX's collectives and lax.ppermute only.
A program may use at most 128 MiB of HBM per device.

```python
import jax
import jax.numpy as jnp
from jax import lax

C = 256
NB = 9
POLAR = 8
LON_DEV = 32
WMAX = 64
NEAR = 16
NLAT = 768
NLON = 1024
N_LON = 32


def draw_widths(key, part):
    first_key = jax.random.fold_in(key, 11)
    second_key = jax.random.fold_in(key, 23)
    rows = jnp.arange(NLAT).astype(jnp.int32)
    distance = jnp.minimum(rows, NLAT - 1 - rows)
    far_width = WMAX - jax.random.randint(first_key, (NLAT,), 0, LON_DEV)
    far_width = jnp.where(distance == 0, WMAX, far_width)
    near_width = jax.random.randint(second_key, (NLAT,), 1, NEAR + 1)
    near_width = jnp.where(rows == POLAR, NEAR, near_width)
    return jnp.where(distance < POLAR, far_width, near_width).astype(jnp.int32)


def with_ends(entries, stream_key, smallest, largest):
    extent = entries.shape
    spot = [jax.random.randint(jax.random.fold_in(stream_key, axis), (), 0, extent[axis]) for axis in range(len(extent))]
    entries = entries.at[tuple(spot)].set(smallest)
    longest = extent.index(max(extent))
    spot[longest] = (spot[longest] + 1) % extent[longest]
    return entries.at[tuple(spot)].set(largest)


def block_scale(key, dims, cuts, least, high):
    loudness = 1.0
    for position, parts in cuts:
        heights = jax.random.uniform(jax.random.fold_in(jax.random.fold_in(key, 6), position), (parts,), jnp.float32, least / len(cuts), high / len(cuts))
        loudness = loudness * jnp.repeat(jnp.exp(heights), dims[position] // parts).reshape((-1,) + (1,) * (len(dims) - 1 - position))
    return loudness


def centred(stream_key, dims, spread, limit, shards=(), held_as=jnp.bfloat16):
    values = spread * jax.random.normal(stream_key, dims, jnp.float32)
    if shards:
        values = values * block_scale(stream_key, dims, shards, -0.22, 0.18)
    return jnp.clip(values, -limit, limit).astype(held_as)


def setup_inputs(seed: int = 0) -> dict:
    arg_keys = jax.random.split(jax.random.key(seed), 6)
    features = centred(arg_keys[0], (NLAT, NLON, C), 1.0, 6.0, ((0, 8), (1, 32)))
    quad_weights = centred(arg_keys[1], (NLAT, 3, 2 * WMAX + 1), 1.0, 6.0, ((0, 8),), jnp.float32)
    cycle_index = with_ends(jax.random.randint(arg_keys[2], (NLAT, 3, 2 * WMAX + 1), 0, NB), jax.random.fold_in(arg_keys[2], 1), 0, NB - 1).astype(jnp.int32)
    widths = draw_widths(jax.random.fold_in(arg_keys[5], 71), 0)
    mix_weight = centred(arg_keys[4], (NB, C, C), (NB * C) ** -0.5, 0.125)
    return dict(features=features, quad_weights=quad_weights, cycle_index=cycle_index, widths=widths, mix_weight=mix_weight)


def basis_table(quad_weights, cycle_index, widths, count):
    offsets = jnp.arange(quad_weights.shape[2]).astype(jnp.int32) - quad_weights.shape[2] // 2
    inside = jnp.abs(offsets)[None, None, :] <= widths[:, None, None]
    member = cycle_index[:, None, :, :] == jnp.arange(count).astype(jnp.int32)[None, :, None, None]
    scale_row = 1.0 / jnp.sqrt(3.0 * (2.0 * widths.astype(jnp.float32) + 1.0))
    values = jnp.where(member & inside[:, None, :, :], quad_weights[:, None, :, :], jnp.float32(0.0))
    return (values * scale_row[:, None, None, None]).astype(jnp.bfloat16)

def toeplitz(values, columns):
    length = values.shape[-1]
    width_all = length - 1 + columns
    padded_values = jnp.concatenate([values, jnp.zeros(values.shape[:-1] + (columns,), values.dtype)], -1)
    tiled = jnp.tile(padded_values, (1,) * (values.ndim - 1) + (columns,))
    flat = tiled[..., :columns * width_all]
    return flat.reshape(values.shape[:-1] + (columns, width_all))

def reference(features, quad_weights, cycle_index, widths, mix_weight):
    count = mix_weight.shape[0]
    basis_values = basis_table(quad_weights, cycle_index, widths, count)
    padded = jnp.pad(features, ((1, 1), (0, 0), (0, 0)))
    weights_wide = mix_weight.astype(jnp.float32)

    def make_row(span):

        def row_out(row):
            rows_three = lax.dynamic_slice_in_dim(padded, row, 3, 0)
            values = lax.dynamic_index_in_dim(basis_values, row, 0, keepdims=False)
            values = values[:, :, WMAX - span:WMAX + span + 1]
            extended = jnp.concatenate([rows_three[:, NLON - span:], rows_three, rows_three[:, :span]], 1)
            starts = (jnp.arange(N_LON) * LON_DEV).astype(jnp.int32)
            index_grid = starts[:, None] + jnp.arange(LON_DEV + 2 * span).astype(jnp.int32)[None, :]
            windows = extended[:, index_grid]
            kernel = toeplitz(values, LON_DEV)
            conv = jnp.einsum('brjm,rnmc->nbjc', kernel.astype(jnp.float32), windows.astype(jnp.float32))
            conv = conv.astype(jnp.bfloat16)
            conv = jnp.transpose(conv, (1, 0, 2, 3)).reshape(count, NLON, C)
            result = rows_three[1].astype(jnp.float32) + jnp.einsum('bjc,bcd->jd', conv.astype(jnp.float32), weights_wide)
            return result.astype(jnp.bfloat16)
        return row_out
    top_rows = lax.map(make_row(WMAX), jnp.arange(POLAR).astype(jnp.int32))
    middle_rows = lax.map(make_row(NEAR), (jnp.arange(NLAT - 2 * POLAR) + POLAR).astype(jnp.int32))
    bottom_rows = lax.map(make_row(WMAX), (jnp.arange(POLAR) + NLAT - POLAR).astype(jnp.int32))
    return jnp.concatenate([top_rows, middle_rows, bottom_rows], 0)
```

```python
import jax
import jax.numpy as jnp
from jax import lax
from jax.sharding import PartitionSpec as P

POLAR = 8
NEAR = 16


def shifted(block, axis, distance):
    devices = range(lax.axis_size(axis))
    route = [((i - distance) % len(devices), i) for i in devices]
    return lax.ppermute(block, axis, route)


def lat_extended(value):
    count, length = lax.axis_size("lat"), value.shape[0]
    up = [(i, i + 1) for i in range(count - 1)]
    down = [(j, i) for i, j in up]
    before = lax.ppermute(value[length - 1 :], "lat", up)
    after = lax.ppermute(value[:1], "lat", down)
    return jnp.concatenate([before, value, after], axis=0)


def basis_table(quad_weights, cycle_index, widths, count):
    offsets = jnp.arange(quad_weights.shape[2]) - quad_weights.shape[2] // 2
    inside = jnp.abs(offsets)[None, None, :] <= widths[:, None, None]
    member = cycle_index[:, None, :, :] == jnp.arange(count)[None, :, None, None]
    scale_row = 1.0 / jnp.sqrt(3.0 * (2.0 * widths.astype(jnp.float32) + 1.0))
    values = jnp.where(
        member & inside[:, None, :, :], quad_weights[:, None, :, :], jnp.float32(0.0)
    )
    return (values * scale_row[:, None, None, None]).astype(jnp.bfloat16)


def shift_table(taps, columns):
    out_pos = jnp.arange(columns)[:, None, None]
    in_pos = jnp.arange(taps - 1 + columns)[None, :, None]
    offset = jnp.arange(taps)[None, None, :]
    return (in_pos - out_pos == offset).astype(jnp.bfloat16)


def conv_rows(extended, values):
    rows, taps = values.shape[0], values.shape[-1]
    columns = extended.shape[1] - (taps - 1)
    kernel = jnp.einsum(
        "nbrk,jmk->njbrm", values, shift_table(taps, columns),
        preferred_element_type=jnp.float32,
    ).astype(jnp.bfloat16)
    stacked = jnp.stack([extended[r : r + rows] for r in range(3)], axis=1)
    return jnp.einsum(
        "njbrm,nrmc->njbc", kernel, stacked, preferred_element_type=jnp.float32
    )


def body(features, quad_weights, cycle_index, widths, mix_weight):
    count = mix_weight.shape[0]
    lat_rows, columns = features.shape[0], features.shape[1]
    reach = quad_weights.shape[2] // 2
    basis_values = basis_table(quad_weights, cycle_index, widths, count)
    padded = lat_extended(features)

    near = jnp.concatenate(
        [shifted(padded[:, columns - NEAR :], "lon", 1), padded,
         shifted(padded[:, :NEAR], "lon", -1)], axis=1)
    conv = conv_rows(near, basis_values[:, :, :, reach - NEAR : reach + NEAR + 1])

    last_band = lax.axis_index("lat") == lax.axis_size("lat") - 1
    start = jnp.where(last_band, lat_rows - POLAR, 0)
    window = lax.dynamic_slice_in_dim(padded, start, POLAR + 2, 0)
    hops = reach // columns
    western = [shifted(window, "lon", hop) for hop in range(hops, 0, -1)]
    eastern = [shifted(window, "lon", -hop) for hop in range(1, hops + 1)]
    wide = jnp.concatenate(western + [window] + eastern, axis=1)
    wide = wide[:, hops * columns - reach : hops * columns + columns + reach]
    polar_values = lax.dynamic_slice_in_dim(basis_values, start, POLAR, 0)
    polar_conv = conv_rows(wide, polar_values)
    conv = lax.dynamic_update_slice_in_dim(conv, polar_conv, start, 0)

    conv = conv.astype(jnp.bfloat16).reshape(lat_rows * columns, -1)
    mixing = jnp.dot(conv, mix_weight.reshape(-1, mix_weight.shape[-1]),
                     preferred_element_type=jnp.float32)
    mixing = mixing.reshape(features.shape)
    return (features.astype(jnp.float32) + mixing).astype(jnp.bfloat16)


def solution(mesh):
    in_specs = (P("lat", "lon", None), P("lat", None, None), P("lat", None, None), P("lat"), P())
    out_specs = P("lat", "lon", None)
    return jax.shard_map(body, mesh=mesh, in_specs=in_specs, out_specs=out_specs, check_vma=False)
```

```python
import functools

import jax
import jax.numpy as jnp
from jax import lax
from jax.experimental import pallas as pl
from jax.experimental.pallas import tpu as pltpu
from jax.sharding import PartitionSpec as P

POLAR = 8
NEAR = 16
BLOCK = 8


def shifted(block, axis, distance):
    devices = range(lax.axis_size(axis))
    route = [((i - distance) % len(devices), i) for i in devices]
    return lax.ppermute(block, axis, route)


def lat_extended(value):
    count, length = lax.axis_size("lat"), value.shape[0]
    up = [(i, i + 1) for i in range(count - 1)]
    down = [(j, i) for i, j in up]
    before = lax.ppermute(value[length - 1 :], "lat", up)
    after = lax.ppermute(value[:1], "lat", down)
    return jnp.concatenate([before, value, after], axis=0)


def basis_table(quad_weights, cycle_index, widths, count):
    offsets = jnp.arange(quad_weights.shape[2]) - quad_weights.shape[2] // 2
    inside = jnp.abs(offsets)[None, None, :] <= widths[:, None, None]
    member = cycle_index[:, None, :, :] == jnp.arange(count)[None, :, None, None]
    scale_row = 1.0 / jnp.sqrt(3.0 * (2.0 * widths.astype(jnp.float32) + 1.0))
    values = jnp.where(
        member & inside[:, None, :, :], quad_weights[:, None, :, :], jnp.float32(0.0)
    )
    return (values * scale_row[:, None, None, None]).astype(jnp.bfloat16)


def toeplitz_stacked(values, columns):
    rows, count, offsets, taps = values.shape
    span = columns + taps - 1
    out_pos = jnp.arange(columns)[:, None, None, None, None]
    in_row = jnp.arange(offsets)[None, :, None, None, None]
    in_pos = jnp.arange(span)[None, None, :, None, None]
    tap_row = jnp.arange(offsets)[None, None, None, :, None]
    tap = jnp.arange(taps)[None, None, None, None, :]
    table = ((in_row == tap_row) & (in_pos - out_pos == tap)).astype(jnp.bfloat16)
    table = table.reshape(columns, offsets * span, offsets * taps)
    kernel = jnp.einsum(
        "nbs,jps->nbjp", values.reshape(rows, count, offsets * taps), table,
        preferred_element_type=jnp.float32,
    ).astype(jnp.bfloat16)
    return kernel.reshape(rows, count * columns, offsets * span)


def toeplitz_split(values, columns):
    rows, count, offsets, taps = values.shape
    span = columns + taps - 1
    out_pos = jnp.arange(columns)[:, None, None]
    in_pos = jnp.arange(span)[None, :, None]
    tap = jnp.arange(taps)[None, None, :]
    table = (in_pos - out_pos == tap).astype(jnp.bfloat16)
    kernel = jnp.einsum(
        "nbrk,jmk->nbjrm", values, table, preferred_element_type=jnp.float32
    ).astype(jnp.bfloat16)
    return kernel.reshape(rows, count * columns, offsets * span)


def conv_mix_kernel(start_ref, ext_ref, k_ref, f_ref, w_ref, *rest):
    o_ref, conv_scr = rest[-2], rest[-1]
    rows, columns, channels = f_ref.shape
    count = w_ref.shape[0]
    span = ext_ref.shape[1]
    base = pl.program_id(0) * rows
    for q in range(rows):
        window = ext_ref[pl.ds(base + q, 3)].reshape(3 * span, channels)
        conv = jnp.dot(k_ref[q], window, preferred_element_type=jnp.float32)
        conv = conv.astype(jnp.bfloat16)
        for b in range(count):
            conv_scr[b, q * columns : (q + 1) * columns, :] = conv[b * columns : (b + 1) * columns]
    acc = f_ref[...].reshape(rows * columns, channels).astype(jnp.float32)
    for b in range(count):
        acc = acc + jnp.dot(conv_scr[b], w_ref[b], preferred_element_type=jnp.float32)
    o_ref[...] = acc.reshape(rows, columns, channels).astype(o_ref.dtype)


def conv_mix(start, extended, kernel, features, mix_weight, previous=None):
    lat_rows, columns, channels = features.shape
    count = mix_weight.shape[0]
    rows = kernel.shape[0]
    blocks = rows // BLOCK
    if previous is None:
        row_map = lambda i, s: (i, 0, 0)
    else:
        row_map = lambda i, s: (s[0] // BLOCK + i, 0, 0)
    in_specs = [
        pl.BlockSpec(extended.shape, lambda i, s: (0, 0, 0)),
        pl.BlockSpec((BLOCK,) + kernel.shape[1:], lambda i, s: (i, 0, 0)),
        pl.BlockSpec((BLOCK, columns, channels), row_map),
        pl.BlockSpec(mix_weight.shape, lambda i, s: (0, 0, 0)),
    ]
    operands = [start, extended, kernel, features, mix_weight]
    aliases = {}
    if previous is not None:
        in_specs.append(pl.BlockSpec(memory_space=pl.ANY))
        operands.append(previous)
        aliases = {len(operands) - 1: 0}
    grid_spec = pltpu.PrefetchScalarGridSpec(
        num_scalar_prefetch=1,
        grid=(blocks,),
        in_specs=in_specs,
        out_specs=pl.BlockSpec((BLOCK, columns, channels), row_map),
        scratch_shapes=[pltpu.VMEM((count, BLOCK * columns, channels), jnp.bfloat16)],
    )
    return pl.pallas_call(
        conv_mix_kernel,
        grid_spec=grid_spec,
        out_shape=jax.ShapeDtypeStruct(features.shape, features.dtype),
        input_output_aliases=aliases,
    )(*operands)


def body(features, quad_weights, cycle_index, widths, mix_weight):
    count = mix_weight.shape[0]
    lat_rows, columns = features.shape[0], features.shape[1]
    reach = quad_weights.shape[2] // 2
    basis_values = basis_table(quad_weights, cycle_index, widths, count)
    padded = lat_extended(features)

    last_band = lax.axis_index("lat") == lax.axis_size("lat") - 1
    start = jnp.where(last_band, lat_rows - POLAR, 0).astype(jnp.int32)
    start_arr = start.reshape(1)

    near = jnp.concatenate(
        [shifted(padded[:, columns - NEAR :], "lon", 1), padded,
         shifted(padded[:, :NEAR], "lon", -1)], axis=1)
    near_kernel = toeplitz_stacked(basis_values[:, :, :, reach - NEAR : reach + NEAR + 1], columns)
    out = conv_mix(start_arr, near, near_kernel, features, mix_weight)

    window = lax.dynamic_slice_in_dim(padded, start, POLAR + 2, 0)
    hops = reach // columns
    western = [shifted(window, "lon", hop) for hop in range(hops, 0, -1)]
    eastern = [shifted(window, "lon", -hop) for hop in range(1, hops + 1)]
    wide = jnp.concatenate(western + [window] + eastern, axis=1)
    wide = wide[:, hops * columns - reach : hops * columns + columns + reach]
    polar_values = lax.dynamic_slice_in_dim(basis_values, start, POLAR, 0)
    wide_kernel = toeplitz_split(polar_values, columns)
    return conv_mix(start_arr, wide, wide_kernel, features, mix_weight, previous=out)


def solution(mesh):
    in_specs = (P("lat", "lon", None), P("lat", None, None), P("lat", None, None), P("lat"), P())
    out_specs = P("lat", "lon", None)
    return jax.shard_map(body, mesh=mesh, in_specs=in_specs, out_specs=out_specs, check_vma=False)
```

```python
import functools

import jax
import jax.numpy as jnp
from jax import lax
from jax.experimental import pallas as pl
from jax.experimental.pallas import tpu as pltpu
from jax.sharding import PartitionSpec as P

POLAR = 8
NEAR = 16
BLOCK = 8


def shifted(block, axis, distance):
    devices = range(lax.axis_size(axis))
    route = [((i - distance) % len(devices), i) for i in devices]
    return lax.ppermute(block, axis, route)


def lat_extended(value):
    count, length = lax.axis_size("lat"), value.shape[0]
    up = [(i, i + 1) for i in range(count - 1)]
    down = [(j, i) for i, j in up]
    before = lax.ppermute(value[length - 1 :], "lat", up)
    after = lax.ppermute(value[:1], "lat", down)
    return jnp.concatenate([before, value, after], axis=0)


def basis_table(quad_weights, cycle_index, widths, count):
    offsets = jnp.arange(quad_weights.shape[2]) - quad_weights.shape[2] // 2
    inside = jnp.abs(offsets)[None, None, :] <= widths[:, None, None]
    member = cycle_index[:, None, :, :] == jnp.arange(count)[None, :, None, None]
    scale_row = 1.0 / jnp.sqrt(3.0 * (2.0 * widths.astype(jnp.float32) + 1.0))
    values = jnp.where(
        member & inside[:, None, :, :], quad_weights[:, None, :, :], jnp.float32(0.0)
    )
    return (values * scale_row[:, None, None, None]).astype(jnp.bfloat16)


def rolled_sources(values, span, lanes):
    rows, count, offsets, taps = values.shape
    columns = span - (taps - 1)
    flat = jnp.pad(values, ((0, 0), (0, 0), (0, 0), (0, span - taps)))
    flat = flat.reshape(rows, count, offsets * span)
    flat = jnp.pad(flat, ((0, 0), (0, 0), (0, lanes - offsets * span))).astype(jnp.float32)
    index = (jnp.arange(lanes)[None, :] + columns * jnp.arange(count)[:, None]) % lanes
    return jnp.take_along_axis(flat, jnp.broadcast_to(index[None], flat.shape), axis=2)


def conv_mix_kernel(start_ref, ext_ref, src_ref, f_ref, w_ref, *rest):
    o_ref, conv_scr = rest[-2], rest[-1]
    rows, columns, channels = f_ref.shape
    count, lanes = src_ref.shape[1], src_ref.shape[2]
    span = ext_ref.shape[1]
    base = pl.program_id(0) * rows
    for q in range(rows):
        source = src_ref[q]
        spread = jnp.broadcast_to(source[:, None, :], (count, columns, lanes))
        spread = spread.reshape(count * columns, lanes)
        kernel = pltpu.roll(spread, 0, 1, stride=1, stride_axis=0).astype(jnp.bfloat16)
        window = ext_ref[pl.ds(base + q, 4)].reshape(4 * span, channels)[:lanes]
        conv = jnp.dot(kernel, window, preferred_element_type=jnp.float32)
        conv = conv.astype(jnp.bfloat16)
        for b in range(count):
            conv_scr[b, q * columns : (q + 1) * columns, :] = conv[b * columns : (b + 1) * columns]
    acc = f_ref[...].reshape(rows * columns, channels).astype(jnp.float32)
    for b in range(count):
        acc = acc + jnp.dot(conv_scr[b], w_ref[b], preferred_element_type=jnp.float32)
    o_ref[...] = acc.reshape(rows, columns, channels).astype(o_ref.dtype)


def conv_mix(start, extended, sources, features, mix_weight, previous=None):
    lat_rows, columns, channels = features.shape
    count = mix_weight.shape[0]
    rows = sources.shape[0]
    blocks = rows // BLOCK
    if previous is None:
        row_map = lambda i, s: (i, 0, 0)
    else:
        row_map = lambda i, s: (s[0] // BLOCK + i, 0, 0)
    in_specs = [
        pl.BlockSpec(extended.shape, lambda i, s: (0, 0, 0)),
        pl.BlockSpec((BLOCK,) + sources.shape[1:], lambda i, s: (i, 0, 0)),
        pl.BlockSpec((BLOCK, columns, channels), row_map),
        pl.BlockSpec(mix_weight.shape, lambda i, s: (0, 0, 0)),
    ]
    operands = [start, extended, sources, features, mix_weight]
    aliases = {}
    if previous is not None:
        in_specs.append(pl.BlockSpec(memory_space=pl.ANY))
        operands.append(previous)
        aliases = {len(operands) - 1: 0}
    grid_spec = pltpu.PrefetchScalarGridSpec(
        num_scalar_prefetch=1,
        grid=(blocks,),
        in_specs=in_specs,
        out_specs=pl.BlockSpec((BLOCK, columns, channels), row_map),
        scratch_shapes=[pltpu.VMEM((count, BLOCK * columns, channels), jnp.bfloat16)],
    )
    return pl.pallas_call(
        conv_mix_kernel,
        grid_spec=grid_spec,
        out_shape=jax.ShapeDtypeStruct(features.shape, features.dtype),
        input_output_aliases=aliases,
    )(*operands)


def body(features, quad_weights, cycle_index, widths, mix_weight):
    count = mix_weight.shape[0]
    lat_rows, columns = features.shape[0], features.shape[1]
    reach = quad_weights.shape[2] // 2
    basis_values = basis_table(quad_weights, cycle_index, widths, count)
    padded = lat_extended(features)

    last_band = lax.axis_index("lat") == lax.axis_size("lat") - 1
    start = jnp.where(last_band, lat_rows - POLAR, 0).astype(jnp.int32)
    start_arr = start.reshape(1)

    near = jnp.concatenate(
        [shifted(padded[:, columns - NEAR :], "lon", 1), padded,
         shifted(padded[:, :NEAR], "lon", -1)], axis=1)
    near = jnp.pad(near, ((0, 1), (0, 0), (0, 0)))
    near_sources = rolled_sources(
        basis_values[:, :, :, reach - NEAR : reach + NEAR + 1], columns + 2 * NEAR, 256)
    out = conv_mix(start_arr, near, near_sources, features, mix_weight)

    window = lax.dynamic_slice_in_dim(padded, start, POLAR + 2, 0)
    hops = reach // columns
    western = [shifted(window, "lon", hop) for hop in range(hops, 0, -1)]
    eastern = [shifted(window, "lon", -hop) for hop in range(1, hops + 1)]
    wide = jnp.concatenate(western + [window] + eastern, axis=1)
    wide = wide[:, hops * columns - reach : hops * columns + columns + reach]
    polar_values = lax.dynamic_slice_in_dim(basis_values, start, POLAR, 0)
    wide = jnp.pad(wide, ((0, 1), (0, 0), (0, 0)))
    wide_sources = rolled_sources(polar_values, columns + 2 * reach, 512)
    return conv_mix(start_arr, wide, wide_sources, features, mix_weight, previous=out)


def solution(mesh):
    in_specs = (P("lat", "lon", None), P("lat", None, None), P("lat", None, None), P("lat"), P())
    out_specs = P("lat", "lon", None)
    return jax.shard_map(body, mesh=mesh, in_specs=in_specs, out_specs=out_specs, check_vma=False)
```

```python
import functools

import jax
import jax.numpy as jnp
from jax import lax
from jax.experimental import pallas as pl
from jax.experimental.pallas import tpu as pltpu
from jax.sharding import PartitionSpec as P

POLAR = 8
NEAR = 16
BLOCK = 8


def shifted(block, axis, distance):
    devices = range(lax.axis_size(axis))
    route = [((i - distance) % len(devices), i) for i in devices]
    return lax.ppermute(block, axis, route)


def lat_extended(value):
    count, length = lax.axis_size("lat"), value.shape[0]
    up = [(i, i + 1) for i in range(count - 1)]
    down = [(j, i) for i, j in up]
    before = lax.ppermute(value[length - 1 :], "lat", up)
    after = lax.ppermute(value[:1], "lat", down)
    return jnp.concatenate([before, value, after], axis=0)


def basis_table(quad_weights, cycle_index, widths, count):
    offsets = jnp.arange(quad_weights.shape[2]) - quad_weights.shape[2] // 2
    inside = jnp.abs(offsets)[None, None, :] <= widths[:, None, None]
    member = cycle_index[:, None, :, :] == jnp.arange(count)[None, :, None, None]
    scale_row = 1.0 / jnp.sqrt(3.0 * (2.0 * widths.astype(jnp.float32) + 1.0))
    values = jnp.where(
        member & inside[:, None, :, :], quad_weights[:, None, :, :], jnp.float32(0.0)
    )
    return (values * scale_row[:, None, None, None]).astype(jnp.bfloat16)


def rolled_sources(values, span, lanes):
    rows, count, offsets, taps = values.shape
    columns = span - (taps - 1)
    flat = jnp.pad(values, ((0, 0), (0, 0), (0, 0), (0, span - taps)))
    flat = flat.reshape(rows, count, offsets * span)
    flat = jnp.pad(flat, ((0, 0), (0, 0), (0, lanes - offsets * span))).astype(jnp.float32)
    return jnp.stack(
        [jnp.roll(flat[:, b], -columns * b, axis=-1) for b in range(count)], axis=1)


def conv_mix_kernel(start_ref, ext_ref, src_ref, f_ref, w_ref, *rest):
    o_ref, conv_scr = rest[-2], rest[-1]
    rows, columns, channels = f_ref.shape
    count, lanes = src_ref.shape[1], src_ref.shape[2]
    span = ext_ref.shape[1]
    base = pl.program_id(0) * rows
    for q in range(rows):
        source = src_ref[q]
        spread = jnp.broadcast_to(source[:, None, :], (count, columns, lanes))
        spread = spread.reshape(count * columns, lanes)
        kernel = pltpu.roll(spread, 0, 1, stride=1, stride_axis=0).astype(jnp.bfloat16)
        window = ext_ref[pl.ds(base + q, 4)].reshape(4 * span, channels)[:lanes]
        conv = jnp.dot(kernel, window, preferred_element_type=jnp.float32)
        conv = conv.astype(jnp.bfloat16)
        for b in range(count):
            conv_scr[b, q * columns : (q + 1) * columns, :] = conv[b * columns : (b + 1) * columns]
    acc = f_ref[...].reshape(rows * columns, channels).astype(jnp.float32)
    for b in range(count):
        acc = acc + jnp.dot(conv_scr[b], w_ref[b], preferred_element_type=jnp.float32)
    o_ref[...] = acc.reshape(rows, columns, channels).astype(o_ref.dtype)


def conv_mix(start, extended, sources, features, mix_weight, previous=None):
    lat_rows, columns, channels = features.shape
    count = mix_weight.shape[0]
    rows = sources.shape[0]
    blocks = rows // BLOCK
    if previous is None:
        row_map = lambda i, s: (i, 0, 0)
    else:
        row_map = lambda i, s: (s[0] // BLOCK + i, 0, 0)
    in_specs = [
        pl.BlockSpec(extended.shape, lambda i, s: (0, 0, 0)),
        pl.BlockSpec((BLOCK,) + sources.shape[1:], lambda i, s: (i, 0, 0)),
        pl.BlockSpec((BLOCK, columns, channels), row_map),
        pl.BlockSpec(mix_weight.shape, lambda i, s: (0, 0, 0)),
    ]
    operands = [start, extended, sources, features, mix_weight]
    aliases = {}
    if previous is not None:
        in_specs.append(pl.BlockSpec(memory_space=pl.ANY))
        operands.append(previous)
        aliases = {len(operands) - 1: 0}
    grid_spec = pltpu.PrefetchScalarGridSpec(
        num_scalar_prefetch=1,
        grid=(blocks,),
        in_specs=in_specs,
        out_specs=pl.BlockSpec((BLOCK, columns, channels), row_map),
        scratch_shapes=[pltpu.VMEM((count, BLOCK * columns, channels), jnp.bfloat16)],
    )
    return pl.pallas_call(
        conv_mix_kernel,
        grid_spec=grid_spec,
        out_shape=jax.ShapeDtypeStruct(features.shape, features.dtype),
        input_output_aliases=aliases,
    )(*operands)


def body(features, quad_weights, cycle_index, widths, mix_weight):
    count = mix_weight.shape[0]
    lat_rows, columns = features.shape[0], features.shape[1]
    reach = quad_weights.shape[2] // 2
    basis_values = basis_table(quad_weights, cycle_index, widths, count)
    padded = lat_extended(features)

    last_band = lax.axis_index("lat") == lax.axis_size("lat") - 1
    start = jnp.where(last_band, lat_rows - POLAR, 0).astype(jnp.int32)
    start_arr = start.reshape(1)

    near = jnp.concatenate(
        [shifted(padded[:, columns - NEAR :], "lon", 1), padded,
         shifted(padded[:, :NEAR], "lon", -1)], axis=1)
    near = jnp.pad(near, ((0, 1), (0, 0), (0, 0)))
    near_sources = rolled_sources(
        basis_values[:, :, :, reach - NEAR : reach + NEAR + 1], columns + 2 * NEAR, 256)
    out = conv_mix(start_arr, near, near_sources, features, mix_weight)

    window = lax.dynamic_slice_in_dim(padded, start, POLAR + 2, 0)
    hops = reach // columns
    western = [shifted(window, "lon", hop) for hop in range(hops, 0, -1)]
    eastern = [shifted(window, "lon", -hop) for hop in range(1, hops + 1)]
    wide = jnp.concatenate(western + [window] + eastern, axis=1)
    wide = wide[:, hops * columns - reach : hops * columns + columns + reach]
    polar_values = lax.dynamic_slice_in_dim(basis_values, start, POLAR, 0)
    wide = jnp.pad(wide, ((0, 1), (0, 0), (0, 0)))
    wide_sources = rolled_sources(polar_values, columns + 2 * reach, 512)
    return conv_mix(start_arr, wide, wide_sources, features, mix_weight, previous=out)


def solution(mesh):
    in_specs = (P("lat", "lon", None), P("lat", None, None), P("lat", None, None), P("lat"), P())
    out_specs = P("lat", "lon", None)
    return jax.shard_map(body, mesh=mesh, in_specs=in_specs, out_specs=out_specs, check_vma=False)
```

```python
import functools

import jax
import jax.numpy as jnp
from jax import lax
from jax.experimental import pallas as pl
from jax.experimental.pallas import tpu as pltpu
from jax.sharding import PartitionSpec as P

POLAR = 8
NEAR = 16
BLOCK = 8


def shifted(block, axis, distance):
    devices = range(lax.axis_size(axis))
    route = [((i - distance) % len(devices), i) for i in devices]
    return lax.ppermute(block, axis, route)


def lat_extended(value):
    count, length = lax.axis_size("lat"), value.shape[0]
    up = [(i, i + 1) for i in range(count - 1)]
    down = [(j, i) for i, j in up]
    before = lax.ppermute(value[length - 1 :], "lat", up)
    after = lax.ppermute(value[:1], "lat", down)
    return jnp.concatenate([before, value, after], axis=0)


def basis_table(quad_weights, cycle_index, widths, count):
    offsets = jnp.arange(quad_weights.shape[2]) - quad_weights.shape[2] // 2
    inside = jnp.abs(offsets)[None, None, :] <= widths[:, None, None]
    member = cycle_index[:, None, :, :] == jnp.arange(count)[None, :, None, None]
    scale_row = 1.0 / jnp.sqrt(3.0 * (2.0 * widths.astype(jnp.float32) + 1.0))
    values = jnp.where(
        member & inside[:, None, :, :], quad_weights[:, None, :, :], jnp.float32(0.0)
    )
    return (values * scale_row[:, None, None, None]).astype(jnp.bfloat16)


def rolled_sources(values, span, lanes):
    rows, count, offsets, taps = values.shape
    columns = span - (taps - 1)
    flat = jnp.pad(values, ((0, 0), (0, 0), (0, 0), (0, span - taps)))
    flat = flat.reshape(rows, count, offsets * span)
    flat = jnp.pad(flat, ((0, 0), (0, 0), (0, lanes - offsets * span))).astype(jnp.float32)
    return jnp.stack(
        [jnp.roll(flat[:, b], -columns * b, axis=-1) for b in range(count)], axis=1)


def conv_mix_kernel(start_ref, ext_ref, src_ref, f_ref, w_ref, *rest):
    o_ref, conv_scr = rest[-2], rest[-1]
    rows, columns, channels = f_ref.shape
    count, lanes = src_ref.shape[1], src_ref.shape[2]
    span = ext_ref.shape[1]
    base = pl.program_id(0) * rows

    def compute():
        for q in range(rows):
            source = src_ref[q]
            spread = jnp.broadcast_to(source[:, None, :], (count, columns, lanes))
            spread = spread.reshape(count * columns, lanes)
            kernel = pltpu.roll(spread, 0, 1, stride=1, stride_axis=0).astype(jnp.bfloat16)
            window = ext_ref[pl.ds(base + q, 4)].reshape(4 * span, channels)[:lanes]
            conv = jnp.dot(kernel, window, preferred_element_type=jnp.float32)
            conv = conv.astype(jnp.bfloat16)
            for b in range(count):
                conv_scr[b, q * columns : (q + 1) * columns, :] = conv[b * columns : (b + 1) * columns]
        acc = f_ref[...].reshape(rows * columns, channels).astype(jnp.float32)
        for b in range(count):
            acc = acc + jnp.dot(conv_scr[b], w_ref[b], preferred_element_type=jnp.float32)
        o_ref[...] = acc.reshape(rows, columns, channels).astype(o_ref.dtype)

    if len(rest) == 2:
        compute()
    else:
        previous_ref = rest[0]
        pl.when(start_ref[1] != 0)(compute)

        @pl.when(start_ref[1] == 0)
        def _():
            o_ref[...] = previous_ref[...]


def conv_mix(start, extended, sources, features, mix_weight, previous=None):
    lat_rows, columns, channels = features.shape
    count = mix_weight.shape[0]
    rows = sources.shape[0]
    blocks = rows // BLOCK
    if previous is None:
        row_map = lambda i, s: (i, 0, 0)
    else:
        row_map = lambda i, s: (s[0] // BLOCK + i, 0, 0)
    in_specs = [
        pl.BlockSpec(extended.shape, lambda i, s: (0, 0, 0)),
        pl.BlockSpec((BLOCK,) + sources.shape[1:], lambda i, s: (i, 0, 0)),
        pl.BlockSpec((BLOCK, columns, channels), row_map),
        pl.BlockSpec(mix_weight.shape, lambda i, s: (0, 0, 0)),
    ]
    operands = [start, extended, sources, features, mix_weight]
    aliases = {}
    if previous is not None:
        in_specs.append(pl.BlockSpec((BLOCK, columns, channels), row_map))
        operands.append(previous)
        aliases = {len(operands) - 1: 0}
    grid_spec = pltpu.PrefetchScalarGridSpec(
        num_scalar_prefetch=1,
        grid=(blocks,),
        in_specs=in_specs,
        out_specs=pl.BlockSpec((BLOCK, columns, channels), row_map),
        scratch_shapes=[pltpu.VMEM((count, BLOCK * columns, channels), jnp.bfloat16)],
    )
    return pl.pallas_call(
        conv_mix_kernel,
        grid_spec=grid_spec,
        out_shape=jax.ShapeDtypeStruct(features.shape, features.dtype),
        input_output_aliases=aliases,
    )(*operands)


def body(features, quad_weights, cycle_index, widths, mix_weight):
    count = mix_weight.shape[0]
    lat_rows, columns, channels = features.shape
    reach = quad_weights.shape[2] // 2
    hops = reach // columns

    lat_index, lat_count = lax.axis_index("lat"), lax.axis_size("lat")
    last_band = lat_index == lat_count - 1
    polar = (lat_index == 0) | last_band
    start = jnp.where(last_band, lat_rows - POLAR, 0).astype(jnp.int32)
    scalars = jnp.stack([start, polar.astype(jnp.int32)])

    zero_row = jnp.zeros((1, columns, channels), features.dtype)
    window = lax.dynamic_slice_in_dim(
        jnp.concatenate([zero_row, features, zero_row], axis=0), start, POLAR + 2, 0)
    flat_window = window.reshape(-1, channels)
    near_count = lat_rows * NEAR
    from_west = shifted(jnp.concatenate(
        [features[:, columns - NEAR :].reshape(-1, channels), flat_window]), "lon", 1)
    from_east = shifted(jnp.concatenate(
        [features[:, :NEAR].reshape(-1, channels), flat_window]), "lon", -1)
    west_far = [shifted(window, "lon", hop) for hop in range(hops, 1, -1)]
    east_far = [shifted(window, "lon", -hop) for hop in range(2, hops + 1)]

    basis_values = basis_table(quad_weights, cycle_index, widths, count)
    near_sources = rolled_sources(
        basis_values[:, :, :, reach - NEAR : reach + NEAR + 1], columns + 2 * NEAR, 256)
    polar_values = lax.dynamic_slice_in_dim(basis_values, start, POLAR, 0)
    wide_sources = rolled_sources(polar_values, columns + 2 * reach, 512)

    west_near = from_west[:near_count].reshape(lat_rows, NEAR, channels)
    east_near = from_east[:near_count].reshape(lat_rows, NEAR, channels)
    near = jnp.concatenate([west_near, features, east_near], axis=1)
    near = lat_extended(near)
    near = jnp.pad(near, ((0, 1), (0, 0), (0, 0)))
    out = conv_mix(scalars, near, near_sources, features, mix_weight)

    west_one = from_west[near_count:].reshape(window.shape)
    east_one = from_east[near_count:].reshape(window.shape)
    wide = jnp.concatenate(west_far + [west_one, window, east_one] + east_far, axis=1)
    wide = wide[:, hops * columns - reach : hops * columns + columns + reach]
    wide = jnp.pad(wide, ((0, 1), (0, 0), (0, 0)))
    return conv_mix(scalars, wide, wide_sources, features, mix_weight, previous=out)


def solution(mesh):
    in_specs = (P("lat", "lon", None), P("lat", None, None), P("lat", None, None), P("lat"), P())
    out_specs = P("lat", "lon", None)
    return jax.shard_map(body, mesh=mesh, in_specs=in_specs, out_specs=out_specs, check_vma=False)
```

```python
import functools

import jax
import jax.numpy as jnp
from jax import lax
from jax.experimental import pallas as pl
from jax.experimental.pallas import tpu as pltpu
from jax.sharding import PartitionSpec as P

POLAR = 8
NEAR = 16
BLOCK = 8


def shifted(block, axis, distance):
    devices = range(lax.axis_size(axis))
    route = [((i - distance) % len(devices), i) for i in devices]
    return lax.ppermute(block, axis, route)


def lat_extended(value):
    count, length = lax.axis_size("lat"), value.shape[0]
    up = [(i, i + 1) for i in range(count - 1)]
    down = [(j, i) for i, j in up]
    before = lax.ppermute(value[length - 1 :], "lat", up)
    after = lax.ppermute(value[:1], "lat", down)
    return jnp.concatenate([before, value, after], axis=0)


def basis_table(quad_weights, cycle_index, widths, count):
    offsets = jnp.arange(quad_weights.shape[2]) - quad_weights.shape[2] // 2
    inside = jnp.abs(offsets)[None, None, :] <= widths[:, None, None]
    member = cycle_index[:, None, :, :] == jnp.arange(count)[None, :, None, None]
    scale_row = 1.0 / jnp.sqrt(3.0 * (2.0 * widths.astype(jnp.float32) + 1.0))
    values = jnp.where(
        member & inside[:, None, :, :], quad_weights[:, None, :, :], jnp.float32(0.0)
    )
    return (values * scale_row[:, None, None, None]).astype(jnp.bfloat16)


def flat_sources(values, span, lanes):
    rows, count, offsets, taps = values.shape
    flat = jnp.pad(values, ((0, 0), (0, 0), (0, 0), (0, span - taps)))
    flat = flat.reshape(rows, count, offsets * span)
    return jnp.pad(flat, ((0, 0), (0, 0), (0, lanes - offsets * span)))


def conv_block(ext_ref, src_ref, f_ref, w_ref, o_ref, conv_scr, base):
    rows, columns, channels = f_ref.shape
    count, lanes = src_ref.shape[1], src_ref.shape[2]
    span = ext_ref.shape[1]
    for q in range(rows):
        source = src_ref[q].astype(jnp.float32)
        pieces = []
        for b in range(count):
            spread = jnp.broadcast_to(source[b : b + 1], (columns, lanes))
            pieces.append(pltpu.roll(spread, 0, 1, stride=1, stride_axis=0))
        kernel = jnp.concatenate(pieces, axis=0).astype(jnp.bfloat16)
        window = ext_ref[pl.ds(base + q, 4)].reshape(4 * span, channels)[:lanes]
        conv = jnp.dot(kernel, window, preferred_element_type=jnp.float32)
        conv = conv.astype(jnp.bfloat16)
        for b in range(count):
            conv_scr[b, q * columns : (q + 1) * columns, :] = conv[b * columns : (b + 1) * columns]
    acc = f_ref[...].reshape(rows * columns, channels).astype(jnp.float32)
    for b in range(count):
        acc = acc + jnp.dot(conv_scr[b], w_ref[b], preferred_element_type=jnp.float32)
    o_ref[...] = acc.reshape(rows, columns, channels).astype(o_ref.dtype)


def near_kernel(scalar_ref, src_ref, f_ref, all_ref, west_ref, east_ref, north_ref,
                south_ref, w_ref, o_ref, ext_scr, conv_scr):
    rows, columns, channels = f_ref.shape
    lat_rows = all_ref.shape[0]
    halo = (ext_scr.shape[1] - columns) // 2
    step = pl.program_id(0)
    base = step * rows

    def put(k, row):
        ext_scr[k, :halo] = west_ref[pl.ds(pl.multiple_of(row * halo, halo), halo)]
        ext_scr[k, halo : halo + columns] = all_ref[row]
        ext_scr[k, halo + columns :] = east_ref[pl.ds(pl.multiple_of(row * halo, halo), halo)]

    for k in range(1, rows + 1):
        put(k, base + k - 1)

    @pl.when(step == 0)
    def _():
        ext_scr[0] = north_ref[0]

    @pl.when(step > 0)
    def _():
        put(0, base - 1)

    @pl.when(step == pl.num_programs(0) - 1)
    def _():
        ext_scr[rows + 1] = south_ref[0]

    @pl.when(step < pl.num_programs(0) - 1)
    def _():
        put(rows + 1, jnp.minimum(base + rows, lat_rows - 1))

    ext_scr[rows + 2] = jnp.zeros(ext_scr.shape[1:], ext_scr.dtype)
    conv_block(ext_scr, src_ref, f_ref, w_ref, o_ref, conv_scr, 0)


def wide_kernel(scalar_ref, ext_ref, src_ref, f_ref, w_ref, prev_ref, o_ref, conv_scr):
    @pl.when(scalar_ref[1] != 0)
    def _():
        conv_block(ext_ref, src_ref, f_ref, w_ref, o_ref, conv_scr, 0)

    @pl.when(scalar_ref[1] == 0)
    def _():
        o_ref[...] = prev_ref[...]


def full_spec(shape):
    return pl.BlockSpec(shape, lambda i, s: (0,) * len(shape))


def near_call(scalars, sources, features, west, east, north, south, mix_weight):
    lat_rows, columns, channels = features.shape
    count = mix_weight.shape[0]
    halo = (north.shape[1] - columns) // 2
    row_map = lambda i, s: (i, 0, 0)
    grid_spec = pltpu.PrefetchScalarGridSpec(
        num_scalar_prefetch=1,
        grid=(lat_rows // BLOCK,),
        in_specs=[
            pl.BlockSpec((BLOCK,) + sources.shape[1:], row_map),
            pl.BlockSpec((BLOCK, columns, channels), row_map),
            full_spec(features.shape), full_spec(west.shape), full_spec(east.shape),
            full_spec(north.shape), full_spec(south.shape), full_spec(mix_weight.shape),
        ],
        out_specs=pl.BlockSpec((BLOCK, columns, channels), row_map),
        scratch_shapes=[
            pltpu.VMEM((BLOCK + 3, columns + 2 * halo, channels), features.dtype),
            pltpu.VMEM((count, BLOCK * columns, channels), jnp.bfloat16),
        ],
    )
    return pl.pallas_call(
        near_kernel, grid_spec=grid_spec,
        out_shape=jax.ShapeDtypeStruct(features.shape, features.dtype),
    )(scalars, sources, features, features, west, east, north, south, mix_weight)


def wide_call(scalars, extended, sources, features, mix_weight, previous):
    lat_rows, columns, channels = features.shape
    count = mix_weight.shape[0]
    row_map = lambda i, s: (s[0] // BLOCK + i, 0, 0)
    grid_spec = pltpu.PrefetchScalarGridSpec(
        num_scalar_prefetch=1,
        grid=(sources.shape[0] // BLOCK,),
        in_specs=[
            full_spec(extended.shape),
            pl.BlockSpec((BLOCK,) + sources.shape[1:], lambda i, s: (i, 0, 0)),
            pl.BlockSpec((BLOCK, columns, channels), row_map),
            full_spec(mix_weight.shape),
            pl.BlockSpec((BLOCK, columns, channels), row_map),
        ],
        out_specs=pl.BlockSpec((BLOCK, columns, channels), row_map),
        scratch_shapes=[pltpu.VMEM((count, BLOCK * columns, channels), jnp.bfloat16)],
    )
    return pl.pallas_call(
        wide_kernel, grid_spec=grid_spec,
        out_shape=jax.ShapeDtypeStruct(features.shape, features.dtype),
        input_output_aliases={5: 0},
    )(scalars, extended, sources, features, mix_weight, previous)


def body(features, quad_weights, cycle_index, widths, mix_weight):
    count = mix_weight.shape[0]
    lat_rows, columns, channels = features.shape
    reach = quad_weights.shape[2] // 2
    hops = reach // columns

    lat_index, lat_count = lax.axis_index("lat"), lax.axis_size("lat")
    last_band = lat_index == lat_count - 1
    polar = (lat_index == 0) | last_band
    start = jnp.where(last_band, lat_rows - POLAR, 0).astype(jnp.int32)
    scalars = jnp.stack([start, polar.astype(jnp.int32)])

    zero_row = jnp.zeros((1, columns, channels), features.dtype)
    window = lax.dynamic_slice_in_dim(
        jnp.concatenate([zero_row, features, zero_row], axis=0), start, POLAR + 2, 0)
    flat_window = window.reshape(-1, channels)
    near_count = lat_rows * NEAR
    from_west = shifted(jnp.concatenate(
        [features[:, columns - NEAR :].reshape(-1, channels), flat_window]), "lon", 1)
    from_east = shifted(jnp.concatenate(
        [features[:, :NEAR].reshape(-1, channels), flat_window]), "lon", -1)
    west_far = [shifted(window, "lon", hop) for hop in range(hops, 1, -1)]
    east_far = [shifted(window, "lon", -hop) for hop in range(2, hops + 1)]

    basis_values = basis_table(quad_weights, cycle_index, widths, count)
    near_sources = flat_sources(
        basis_values[:, :, :, reach - NEAR : reach + NEAR + 1], columns + 2 * NEAR, 256)
    polar_values = lax.dynamic_slice_in_dim(basis_values, start, POLAR, 0)
    wide_sources = flat_sources(polar_values, columns + 2 * reach, 512)

    def edge(row):
        return jnp.concatenate(
            [from_west[row * NEAR : (row + 1) * NEAR][None], features[row : row + 1],
             from_east[row * NEAR : (row + 1) * NEAR][None]], axis=1)

    count_lat = lax.axis_size("lat")
    up = [(i, i + 1) for i in range(count_lat - 1)]
    down = [(j, i) for i, j in up]
    north = lax.ppermute(edge(lat_rows - 1), "lat", up)
    south = lax.ppermute(edge(0), "lat", down)
    out = near_call(scalars, near_sources, features, from_west, from_east, north, south,
                    mix_weight)

    west_one = from_west[near_count:].reshape(window.shape)
    east_one = from_east[near_count:].reshape(window.shape)
    wide = jnp.concatenate(west_far + [west_one, window, east_one] + east_far, axis=1)
    wide = wide[:, hops * columns - reach : hops * columns + columns + reach]
    wide = jnp.pad(wide, ((0, 1), (0, 0), (0, 0)))
    return wide_call(scalars, wide, wide_sources, features, mix_weight, out)


def solution(mesh):
    in_specs = (P("lat", "lon", None), P("lat", None, None), P("lat", None, None), P("lat"), P())
    out_specs = P("lat", "lon", None)
    return jax.shard_map(body, mesh=mesh, in_specs=in_specs, out_specs=out_specs, check_vma=False)
```

```python
import functools

import jax
import jax.numpy as jnp
from jax import lax
from jax.experimental import pallas as pl
from jax.experimental.pallas import tpu as pltpu
from jax.sharding import PartitionSpec as P

POLAR = 8
NEAR = 16
BLOCK = 8


def shifted(block, axis, distance):
    devices = range(lax.axis_size(axis))
    route = [((i - distance) % len(devices), i) for i in devices]
    return lax.ppermute(block, axis, route)


def lat_extended(value):
    count, length = lax.axis_size("lat"), value.shape[0]
    up = [(i, i + 1) for i in range(count - 1)]
    down = [(j, i) for i, j in up]
    before = lax.ppermute(value[length - 1 :], "lat", up)
    after = lax.ppermute(value[:1], "lat", down)
    return jnp.concatenate([before, value, after], axis=0)


def basis_table(quad_weights, cycle_index, widths, count):
    offsets = jnp.arange(quad_weights.shape[2]) - quad_weights.shape[2] // 2
    inside = jnp.abs(offsets)[None, None, :] <= widths[:, None, None]
    member = cycle_index[:, None, :, :] == jnp.arange(count)[None, :, None, None]
    scale_row = 1.0 / jnp.sqrt(3.0 * (2.0 * widths.astype(jnp.float32) + 1.0))
    values = jnp.where(
        member & inside[:, None, :, :], quad_weights[:, None, :, :], jnp.float32(0.0)
    )
    return (values * scale_row[:, None, None, None]).astype(jnp.bfloat16)


def flat_sources(values, span, lanes):
    rows, count, offsets, taps = values.shape
    flat = jnp.pad(values, ((0, 0), (0, 0), (0, 0), (0, span - taps)))
    flat = flat.reshape(rows, count, offsets * span)
    return jnp.pad(flat, ((0, 0), (0, 0), (0, lanes - offsets * span)))


def conv_block(ext_ref, src_ref, f_ref, w_ref, o_ref, conv_scr, base):
    rows, columns, channels = f_ref.shape
    count, lanes = src_ref.shape[1], src_ref.shape[2]
    span = ext_ref.shape[1]
    for q in range(rows):
        source = src_ref[q].astype(jnp.float32)
        pieces = []
        for b in range(count):
            spread = jnp.broadcast_to(source[b : b + 1], (columns, lanes))
            pieces.append(pltpu.roll(spread, 0, 1, stride=1, stride_axis=0))
        kernel = jnp.concatenate(pieces, axis=0).astype(jnp.bfloat16)
        window = ext_ref[pl.ds(base + q, 4)].reshape(4 * span, channels)[:lanes]
        conv = jnp.dot(kernel, window, preferred_element_type=jnp.float32)
        conv = conv.astype(jnp.bfloat16)
        for b in range(count):
            conv_scr[b, q * columns : (q + 1) * columns, :] = conv[b * columns : (b + 1) * columns]
    acc = f_ref[...].reshape(rows * columns, channels).astype(jnp.float32)
    for b in range(count):
        acc = acc + jnp.dot(conv_scr[b], w_ref[b], preferred_element_type=jnp.float32)
    o_ref[...] = acc.reshape(rows, columns, channels).astype(o_ref.dtype)


def near_kernel(scalar_ref, src_ref, f_ref, all_ref, west_ref, east_ref, north_ref,
                south_ref, w_ref, o_ref, ext_scr, conv_scr):
    rows, columns, channels = f_ref.shape
    lat_rows = all_ref.shape[0]
    halo = (ext_scr.shape[1] - columns) // 2
    step = pl.program_id(0)
    base = step * rows

    def sides(k, row):
        start = pl.multiple_of((row + 1) * halo, halo)
        ext_scr[k, :halo] = west_ref[pl.ds(start, halo)]
        ext_scr[k, halo + columns :] = east_ref[pl.ds(start, halo)]

    for k in range(rows + 2):
        sides(k, base + k - 1)
    for k in range(1, rows + 1):
        ext_scr[k, halo : halo + columns] = all_ref[base + k - 1]

    @pl.when(step == 0)
    def _():
        ext_scr[0, halo : halo + columns] = north_ref[0]

    @pl.when(step > 0)
    def _():
        ext_scr[0, halo : halo + columns] = all_ref[jnp.maximum(base - 1, 0)]

    @pl.when(step == pl.num_programs(0) - 1)
    def _():
        ext_scr[rows + 1, halo : halo + columns] = south_ref[0]

    @pl.when(step < pl.num_programs(0) - 1)
    def _():
        ext_scr[rows + 1, halo : halo + columns] = all_ref[jnp.minimum(base + rows, lat_rows - 1)]

    ext_scr[rows + 2] = jnp.zeros(ext_scr.shape[1:], ext_scr.dtype)
    conv_block(ext_scr, src_ref, f_ref, w_ref, o_ref, conv_scr, 0)


def wide_kernel(scalar_ref, ext_ref, src_ref, f_ref, w_ref, prev_ref, o_ref, conv_scr):
    @pl.when(scalar_ref[1] != 0)
    def _():
        conv_block(ext_ref, src_ref, f_ref, w_ref, o_ref, conv_scr, 0)

    @pl.when(scalar_ref[1] == 0)
    def _():
        o_ref[...] = prev_ref[...]


def full_spec(shape):
    return pl.BlockSpec(shape, lambda i, s: (0,) * len(shape))


def near_call(scalars, sources, features, west, east, north, south, mix_weight):
    lat_rows, columns, channels = features.shape
    count = mix_weight.shape[0]
    halo = NEAR
    row_map = lambda i, s: (i, 0, 0)
    grid_spec = pltpu.PrefetchScalarGridSpec(
        num_scalar_prefetch=1,
        grid=(lat_rows // BLOCK,),
        in_specs=[
            pl.BlockSpec((BLOCK,) + sources.shape[1:], row_map),
            pl.BlockSpec((BLOCK, columns, channels), row_map),
            full_spec(features.shape), full_spec(west.shape), full_spec(east.shape),
            full_spec(north.shape), full_spec(south.shape), full_spec(mix_weight.shape),
        ],
        out_specs=pl.BlockSpec((BLOCK, columns, channels), row_map),
        scratch_shapes=[
            pltpu.VMEM((BLOCK + 3, columns + 2 * halo, channels), features.dtype),
            pltpu.VMEM((count, BLOCK * columns, channels), jnp.bfloat16),
        ],
    )
    return pl.pallas_call(
        near_kernel, grid_spec=grid_spec,
        out_shape=jax.ShapeDtypeStruct(features.shape, features.dtype),
    )(scalars, sources, features, features, west, east, north, south, mix_weight)


def wide_call(scalars, extended, sources, features, mix_weight, previous):
    lat_rows, columns, channels = features.shape
    count = mix_weight.shape[0]
    row_map = lambda i, s: (s[0] // BLOCK + i, 0, 0)
    grid_spec = pltpu.PrefetchScalarGridSpec(
        num_scalar_prefetch=1,
        grid=(sources.shape[0] // BLOCK,),
        in_specs=[
            full_spec(extended.shape),
            pl.BlockSpec((BLOCK,) + sources.shape[1:], lambda i, s: (i, 0, 0)),
            pl.BlockSpec((BLOCK, columns, channels), row_map),
            full_spec(mix_weight.shape),
            pl.BlockSpec((BLOCK, columns, channels), row_map),
        ],
        out_specs=pl.BlockSpec((BLOCK, columns, channels), row_map),
        scratch_shapes=[pltpu.VMEM((count, BLOCK * columns, channels), jnp.bfloat16)],
    )
    return pl.pallas_call(
        wide_kernel, grid_spec=grid_spec,
        out_shape=jax.ShapeDtypeStruct(features.shape, features.dtype),
        input_output_aliases={5: 0},
    )(scalars, extended, sources, features, mix_weight, previous)


def body(features, quad_weights, cycle_index, widths, mix_weight):
    count = mix_weight.shape[0]
    lat_rows, columns, channels = features.shape
    reach = quad_weights.shape[2] // 2
    hops = reach // columns

    lat_index, lat_count = lax.axis_index("lat"), lax.axis_size("lat")
    last_band = lat_index == lat_count - 1
    polar = (lat_index == 0) | last_band
    start = jnp.where(last_band, lat_rows - POLAR, 0).astype(jnp.int32)
    scalars = jnp.stack([start, polar.astype(jnp.int32)])

    zero_row = jnp.zeros((1, columns, channels), features.dtype)
    window = lax.dynamic_slice_in_dim(
        jnp.concatenate([zero_row, features, zero_row], axis=0), start, POLAR + 2, 0)
    flat_window = window.reshape(-1, channels)
    count_lat = lax.axis_size("lat")
    up = [(i, i + 1) for i in range(count_lat - 1)]
    down = [(j, i) for i, j in up]
    north = lax.ppermute(features[lat_rows - 1 :], "lat", up)
    south = lax.ppermute(features[:1], "lat", down)
    padded = jnp.concatenate([north, features, south], axis=0)
    near_count = (lat_rows + 2) * NEAR
    from_west = shifted(jnp.concatenate(
        [padded[:, columns - NEAR :].reshape(-1, channels), flat_window]), "lon", 1)
    from_east = shifted(jnp.concatenate(
        [padded[:, :NEAR].reshape(-1, channels), flat_window]), "lon", -1)
    west_far = [shifted(window, "lon", hop) for hop in range(hops, 1, -1)]
    east_far = [shifted(window, "lon", -hop) for hop in range(2, hops + 1)]

    basis_values = basis_table(quad_weights, cycle_index, widths, count)
    near_sources = flat_sources(
        basis_values[:, :, :, reach - NEAR : reach + NEAR + 1], columns + 2 * NEAR, 256)
    polar_values = lax.dynamic_slice_in_dim(basis_values, start, POLAR, 0)
    wide_sources = flat_sources(polar_values, columns + 2 * reach, 512)

    out = near_call(scalars, near_sources, features, from_west, from_east, north, south,
                    mix_weight)

    west_one = from_west[near_count:].reshape(window.shape)
    east_one = from_east[near_count:].reshape(window.shape)
    wide = jnp.concatenate(west_far + [west_one, window, east_one] + east_far, axis=1)
    wide = wide[:, hops * columns - reach : hops * columns + columns + reach]
    wide = jnp.pad(wide, ((0, 1), (0, 0), (0, 0)))
    return wide_call(scalars, wide, wide_sources, features, mix_weight, out)


def solution(mesh):
    in_specs = (P("lat", "lon", None), P("lat", None, None), P("lat", None, None), P("lat"), P())
    out_specs = P("lat", "lon", None)
    return jax.shard_map(body, mesh=mesh, in_specs=in_specs, out_specs=out_specs, check_vma=False)
```

```python
import functools

import jax
import jax.numpy as jnp
from jax import lax
from jax.experimental import pallas as pl
from jax.experimental.pallas import tpu as pltpu
from jax.sharding import PartitionSpec as P

POLAR = 8
NEAR = 16
BLOCK = 8
NEAR_BLOCK = 16


def shifted(block, axis, distance):
    devices = range(lax.axis_size(axis))
    route = [((i - distance) % len(devices), i) for i in devices]
    return lax.ppermute(block, axis, route)


def lat_extended(value):
    count, length = lax.axis_size("lat"), value.shape[0]
    up = [(i, i + 1) for i in range(count - 1)]
    down = [(j, i) for i, j in up]
    before = lax.ppermute(value[length - 1 :], "lat", up)
    after = lax.ppermute(value[:1], "lat", down)
    return jnp.concatenate([before, value, after], axis=0)


def basis_table(quad_weights, cycle_index, widths, count):
    offsets = jnp.arange(quad_weights.shape[2]) - quad_weights.shape[2] // 2
    inside = jnp.abs(offsets)[None, None, :] <= widths[:, None, None]
    member = cycle_index[:, None, :, :] == jnp.arange(count)[None, :, None, None]
    scale_row = 1.0 / jnp.sqrt(3.0 * (2.0 * widths.astype(jnp.float32) + 1.0))
    values = jnp.where(
        member & inside[:, None, :, :], quad_weights[:, None, :, :], jnp.float32(0.0)
    )
    return (values * scale_row[:, None, None, None]).astype(jnp.bfloat16)


def flat_sources(values, span, lanes):
    rows, count, offsets, taps = values.shape
    flat = jnp.pad(values, ((0, 0), (0, 0), (0, 0), (0, span - taps)))
    flat = flat.reshape(rows, count, offsets * span)
    return jnp.pad(flat, ((0, 0), (0, 0), (0, lanes - offsets * span)))


def conv_block(ext_ref, src_ref, f_ref, w_ref, o_ref, conv_scr, base):
    rows, columns, channels = f_ref.shape
    count, lanes = src_ref.shape[1], src_ref.shape[2]
    span = ext_ref.shape[1]
    for q in range(rows):
        source = src_ref[q].astype(jnp.float32)
        pieces = []
        for b in range(count):
            spread = jnp.broadcast_to(source[b : b + 1], (columns, lanes))
            pieces.append(pltpu.roll(spread, 0, 1, stride=1, stride_axis=0))
        kernel = jnp.concatenate(pieces, axis=0).astype(jnp.bfloat16)
        window = ext_ref[pl.ds(base + q, 4)].reshape(4 * span, channels)[:lanes]
        conv = jnp.dot(kernel, window, preferred_element_type=jnp.float32)
        conv = conv.astype(jnp.bfloat16)
        for b in range(count):
            conv_scr[b, q * columns : (q + 1) * columns, :] = conv[b * columns : (b + 1) * columns]
    acc = f_ref[...].reshape(rows * columns, channels).astype(jnp.float32)
    for b in range(count):
        acc = acc + jnp.dot(conv_scr[b], w_ref[b], preferred_element_type=jnp.float32)
    o_ref[...] = acc.reshape(rows, columns, channels).astype(o_ref.dtype)


def near_kernel(scalar_ref, src_ref, f_ref, all_ref, west_ref, east_ref, north_ref,
                south_ref, w_ref, o_ref, ext_scr, conv_scr):
    rows, columns, channels = f_ref.shape
    lat_rows = all_ref.shape[0]
    halo = (ext_scr.shape[1] - columns) // 2
    step = pl.program_id(0)
    base = step * rows

    def put(k, row):
        ext_scr[k, :halo] = west_ref[pl.ds(pl.multiple_of(row * halo, halo), halo)]
        ext_scr[k, halo : halo + columns] = all_ref[row]
        ext_scr[k, halo + columns :] = east_ref[pl.ds(pl.multiple_of(row * halo, halo), halo)]

    for k in range(1, rows + 1):
        put(k, base + k - 1)

    @pl.when(step == 0)
    def _():
        ext_scr[0] = north_ref[0]

    @pl.when(step > 0)
    def _():
        put(0, base - 1)

    @pl.when(step == pl.num_programs(0) - 1)
    def _():
        ext_scr[rows + 1] = south_ref[0]

    @pl.when(step < pl.num_programs(0) - 1)
    def _():
        put(rows + 1, jnp.minimum(base + rows, lat_rows - 1))

    ext_scr[rows + 2] = jnp.zeros(ext_scr.shape[1:], ext_scr.dtype)
    conv_block(ext_scr, src_ref, f_ref, w_ref, o_ref, conv_scr, 0)


def wide_kernel(scalar_ref, ext_ref, src_ref, f_ref, w_ref, prev_ref, o_ref, conv_scr):
    @pl.when(scalar_ref[1] != 0)
    def _():
        conv_block(ext_ref, src_ref, f_ref, w_ref, o_ref, conv_scr, 0)

    @pl.when(scalar_ref[1] == 0)
    def _():
        o_ref[...] = prev_ref[...]


def full_spec(shape):
    return pl.BlockSpec(shape, lambda i, s: (0,) * len(shape))


def near_call(scalars, sources, features, west, east, north, south, mix_weight):
    lat_rows, columns, channels = features.shape
    count = mix_weight.shape[0]
    halo = (north.shape[1] - columns) // 2
    row_map = lambda i, s: (i, 0, 0)
    grid_spec = pltpu.PrefetchScalarGridSpec(
        num_scalar_prefetch=1,
        grid=(lat_rows // NEAR_BLOCK,),
        in_specs=[
            pl.BlockSpec((NEAR_BLOCK,) + sources.shape[1:], row_map),
            pl.BlockSpec((NEAR_BLOCK, columns, channels), row_map),
            full_spec(features.shape), full_spec(west.shape), full_spec(east.shape),
            full_spec(north.shape), full_spec(south.shape), full_spec(mix_weight.shape),
        ],
        out_specs=pl.BlockSpec((NEAR_BLOCK, columns, channels), row_map),
        scratch_shapes=[
            pltpu.VMEM((NEAR_BLOCK + 3, columns + 2 * halo, channels), features.dtype),
            pltpu.VMEM((count, NEAR_BLOCK * columns, channels), jnp.bfloat16),
        ],
    )
    return pl.pallas_call(
        near_kernel, grid_spec=grid_spec,
        out_shape=jax.ShapeDtypeStruct(features.shape, features.dtype),
    )(scalars, sources, features, features, west, east, north, south, mix_weight)


def wide_call(scalars, extended, sources, features, mix_weight, previous):
    lat_rows, columns, channels = features.shape
    count = mix_weight.shape[0]
    row_map = lambda i, s: (s[0] // BLOCK + i, 0, 0)
    grid_spec = pltpu.PrefetchScalarGridSpec(
        num_scalar_prefetch=1,
        grid=(sources.shape[0] // BLOCK,),
        in_specs=[
            full_spec(extended.shape),
            pl.BlockSpec((BLOCK,) + sources.shape[1:], lambda i, s: (i, 0, 0)),
            pl.BlockSpec((BLOCK, columns, channels), row_map),
            full_spec(mix_weight.shape),
            pl.BlockSpec((BLOCK, columns, channels), row_map),
        ],
        out_specs=pl.BlockSpec((BLOCK, columns, channels), row_map),
        scratch_shapes=[pltpu.VMEM((count, BLOCK * columns, channels), jnp.bfloat16)],
    )
    return pl.pallas_call(
        wide_kernel, grid_spec=grid_spec,
        out_shape=jax.ShapeDtypeStruct(features.shape, features.dtype),
        input_output_aliases={5: 0},
    )(scalars, extended, sources, features, mix_weight, previous)


def body(features, quad_weights, cycle_index, widths, mix_weight):
    count = mix_weight.shape[0]
    lat_rows, columns, channels = features.shape
    reach = quad_weights.shape[2] // 2
    hops = reach // columns

    lat_index, lat_count = lax.axis_index("lat"), lax.axis_size("lat")
    last_band = lat_index == lat_count - 1
    polar = (lat_index == 0) | last_band
    start = jnp.where(last_band, lat_rows - POLAR, 0).astype(jnp.int32)
    scalars = jnp.stack([start, polar.astype(jnp.int32)])

    zero_row = jnp.zeros((1, columns, channels), features.dtype)
    window = lax.dynamic_slice_in_dim(
        jnp.concatenate([zero_row, features, zero_row], axis=0), start, POLAR + 2, 0)
    flat_window = window.reshape(-1, channels)
    near_count = lat_rows * NEAR
    from_west = shifted(jnp.concatenate(
        [features[:, columns - NEAR :].reshape(-1, channels), flat_window]), "lon", 1)
    from_east = shifted(jnp.concatenate(
        [features[:, :NEAR].reshape(-1, channels), flat_window]), "lon", -1)
    west_far = [shifted(window, "lon", hop) for hop in range(hops, 1, -1)]
    east_far = [shifted(window, "lon", -hop) for hop in range(2, hops + 1)]

    basis_values = basis_table(quad_weights, cycle_index, widths, count)
    near_sources = flat_sources(
        basis_values[:, :, :, reach - NEAR : reach + NEAR + 1], columns + 2 * NEAR, 256)
    polar_values = lax.dynamic_slice_in_dim(basis_values, start, POLAR, 0)
    wide_sources = flat_sources(polar_values, columns + 2 * reach, 512)

    def edge(row):
        return jnp.concatenate(
            [from_west[row * NEAR : (row + 1) * NEAR][None], features[row : row + 1],
             from_east[row * NEAR : (row + 1) * NEAR][None]], axis=1)

    count_lat = lax.axis_size("lat")
    up = [(i, i + 1) for i in range(count_lat - 1)]
    down = [(j, i) for i, j in up]
    north = lax.ppermute(edge(lat_rows - 1), "lat", up)
    south = lax.ppermute(edge(0), "lat", down)
    out = near_call(scalars, near_sources, features, from_west, from_east, north, south,
                    mix_weight)

    west_one = from_west[near_count:].reshape(window.shape)
    east_one = from_east[near_count:].reshape(window.shape)
    wide = jnp.concatenate(west_far + [west_one, window, east_one] + east_far, axis=1)
    wide = wide[:, hops * columns - reach : hops * columns + columns + reach]
    wide = jnp.pad(wide, ((0, 1), (0, 0), (0, 0)))
    return wide_call(scalars, wide, wide_sources, features, mix_weight, out)


def solution(mesh):
    in_specs = (P("lat", "lon", None), P("lat", None, None), P("lat", None, None), P("lat"), P())
    out_specs = P("lat", "lon", None)
    return jax.shard_map(body, mesh=mesh, in_specs=in_specs, out_specs=out_specs, check_vma=False)
```

```python
import functools

import jax
import jax.numpy as jnp
from jax import lax
from jax.experimental import pallas as pl
from jax.experimental.pallas import tpu as pltpu
from jax.sharding import PartitionSpec as P

POLAR = 8
NEAR = 16
BLOCK = 8
NEAR_BLOCK = 32


def shifted(block, axis, distance):
    devices = range(lax.axis_size(axis))
    route = [((i - distance) % len(devices), i) for i in devices]
    return lax.ppermute(block, axis, route)


def lat_extended(value):
    count, length = lax.axis_size("lat"), value.shape[0]
    up = [(i, i + 1) for i in range(count - 1)]
    down = [(j, i) for i, j in up]
    before = lax.ppermute(value[length - 1 :], "lat", up)
    after = lax.ppermute(value[:1], "lat", down)
    return jnp.concatenate([before, value, after], axis=0)


def basis_table(quad_weights, cycle_index, widths, count):
    offsets = jnp.arange(quad_weights.shape[2]) - quad_weights.shape[2] // 2
    inside = jnp.abs(offsets)[None, None, :] <= widths[:, None, None]
    member = cycle_index[:, None, :, :] == jnp.arange(count)[None, :, None, None]
    scale_row = 1.0 / jnp.sqrt(3.0 * (2.0 * widths.astype(jnp.float32) + 1.0))
    values = jnp.where(
        member & inside[:, None, :, :], quad_weights[:, None, :, :], jnp.float32(0.0)
    )
    return (values * scale_row[:, None, None, None]).astype(jnp.bfloat16)


def flat_sources(values, span, lanes):
    rows, count, offsets, taps = values.shape
    flat = jnp.pad(values, ((0, 0), (0, 0), (0, 0), (0, span - taps)))
    flat = flat.reshape(rows, count, offsets * span)
    return jnp.pad(flat, ((0, 0), (0, 0), (0, lanes - offsets * span)))


def conv_block(ext_ref, src_ref, f_ref, w_ref, o_ref, conv_scr, base):
    rows, columns, channels = f_ref.shape
    count, lanes = src_ref.shape[1], src_ref.shape[2]
    span = ext_ref.shape[1]
    for q in range(rows):
        source = src_ref[q].astype(jnp.float32)
        pieces = []
        for b in range(count):
            spread = jnp.broadcast_to(source[b : b + 1], (columns, lanes))
            pieces.append(pltpu.roll(spread, 0, 1, stride=1, stride_axis=0))
        kernel = jnp.concatenate(pieces, axis=0).astype(jnp.bfloat16)
        window = ext_ref[pl.ds(base + q, 4)].reshape(4 * span, channels)[:lanes]
        conv = jnp.dot(kernel, window, preferred_element_type=jnp.float32)
        conv = conv.astype(jnp.bfloat16)
        for b in range(count):
            conv_scr[b, q * columns : (q + 1) * columns, :] = conv[b * columns : (b + 1) * columns]
    acc = f_ref[...].reshape(rows * columns, channels).astype(jnp.float32)
    for b in range(count):
        acc = acc + jnp.dot(conv_scr[b], w_ref[b], preferred_element_type=jnp.float32)
    o_ref[...] = acc.reshape(rows, columns, channels).astype(o_ref.dtype)


def near_kernel(scalar_ref, src_ref, f_ref, all_ref, west_ref, east_ref, north_ref,
                south_ref, w_ref, o_ref, ext_scr, conv_scr):
    rows, columns, channels = f_ref.shape
    lat_rows = all_ref.shape[0]
    halo = (ext_scr.shape[1] - columns) // 2
    step = pl.program_id(0)
    base = step * rows

    def put(k, row):
        ext_scr[k, :halo] = west_ref[pl.ds(pl.multiple_of(row * halo, halo), halo)]
        ext_scr[k, halo : halo + columns] = all_ref[row]
        ext_scr[k, halo + columns :] = east_ref[pl.ds(pl.multiple_of(row * halo, halo), halo)]

    for k in range(1, rows + 1):
        put(k, base + k - 1)

    @pl.when(step == 0)
    def _():
        ext_scr[0] = north_ref[0]

    @pl.when(step > 0)
    def _():
        put(0, base - 1)

    @pl.when(step == pl.num_programs(0) - 1)
    def _():
        ext_scr[rows + 1] = south_ref[0]

    @pl.when(step < pl.num_programs(0) - 1)
    def _():
        put(rows + 1, jnp.minimum(base + rows, lat_rows - 1))

    ext_scr[rows + 2] = jnp.zeros(ext_scr.shape[1:], ext_scr.dtype)
    conv_block(ext_scr, src_ref, f_ref, w_ref, o_ref, conv_scr, 0)


def wide_kernel(scalar_ref, ext_ref, src_ref, f_ref, w_ref, prev_ref, o_ref, conv_scr):
    @pl.when(scalar_ref[1] != 0)
    def _():
        conv_block(ext_ref, src_ref, f_ref, w_ref, o_ref, conv_scr, 0)

    @pl.when(scalar_ref[1] == 0)
    def _():
        o_ref[...] = prev_ref[...]


def full_spec(shape):
    return pl.BlockSpec(shape, lambda i, s: (0,) * len(shape))


def near_call(scalars, sources, features, west, east, north, south, mix_weight):
    lat_rows, columns, channels = features.shape
    count = mix_weight.shape[0]
    halo = (north.shape[1] - columns) // 2
    row_map = lambda i, s: (i, 0, 0)
    grid_spec = pltpu.PrefetchScalarGridSpec(
        num_scalar_prefetch=1,
        grid=(lat_rows // NEAR_BLOCK,),
        in_specs=[
            pl.BlockSpec((NEAR_BLOCK,) + sources.shape[1:], row_map),
            pl.BlockSpec((NEAR_BLOCK, columns, channels), row_map),
            full_spec(features.shape), full_spec(west.shape), full_spec(east.shape),
            full_spec(north.shape), full_spec(south.shape), full_spec(mix_weight.shape),
        ],
        out_specs=pl.BlockSpec((NEAR_BLOCK, columns, channels), row_map),
        scratch_shapes=[
            pltpu.VMEM((NEAR_BLOCK + 3, columns + 2 * halo, channels), features.dtype),
            pltpu.VMEM((count, NEAR_BLOCK * columns, channels), jnp.bfloat16),
        ],
    )
    return pl.pallas_call(
        near_kernel, grid_spec=grid_spec,
        out_shape=jax.ShapeDtypeStruct(features.shape, features.dtype),
    )(scalars, sources, features, features, west, east, north, south, mix_weight)


def wide_call(scalars, extended, sources, features, mix_weight, previous):
    lat_rows, columns, channels = features.shape
    count = mix_weight.shape[0]
    row_map = lambda i, s: (s[0] // BLOCK + i, 0, 0)
    grid_spec = pltpu.PrefetchScalarGridSpec(
        num_scalar_prefetch=1,
        grid=(sources.shape[0] // BLOCK,),
        in_specs=[
            full_spec(extended.shape),
            pl.BlockSpec((BLOCK,) + sources.shape[1:], lambda i, s: (i, 0, 0)),
            pl.BlockSpec((BLOCK, columns, channels), row_map),
            full_spec(mix_weight.shape),
            pl.BlockSpec((BLOCK, columns, channels), row_map),
        ],
        out_specs=pl.BlockSpec((BLOCK, columns, channels), row_map),
        scratch_shapes=[pltpu.VMEM((count, BLOCK * columns, channels), jnp.bfloat16)],
    )
    return pl.pallas_call(
        wide_kernel, grid_spec=grid_spec,
        out_shape=jax.ShapeDtypeStruct(features.shape, features.dtype),
        input_output_aliases={5: 0},
    )(scalars, extended, sources, features, mix_weight, previous)


def body(features, quad_weights, cycle_index, widths, mix_weight):
    count = mix_weight.shape[0]
    lat_rows, columns, channels = features.shape
    reach = quad_weights.shape[2] // 2
    hops = reach // columns

    lat_index, lat_count = lax.axis_index("lat"), lax.axis_size("lat")
    last_band = lat_index == lat_count - 1
    polar = (lat_index == 0) | last_band
    start = jnp.where(last_band, lat_rows - POLAR, 0).astype(jnp.int32)
    scalars = jnp.stack([start, polar.astype(jnp.int32)])

    zero_row = jnp.zeros((1, columns, channels), features.dtype)
    window = lax.dynamic_slice_in_dim(
        jnp.concatenate([zero_row, features, zero_row], axis=0), start, POLAR + 2, 0)
    flat_window = window.reshape(-1, channels)
    near_count = lat_rows * NEAR
    from_west = shifted(jnp.concatenate(
        [features[:, columns - NEAR :].reshape(-1, channels), flat_window]), "lon", 1)
    from_east = shifted(jnp.concatenate(
        [features[:, :NEAR].reshape(-1, channels), flat_window]), "lon", -1)
    west_far = [shifted(window, "lon", hop) for hop in range(hops, 1, -1)]
    east_far = [shifted(window, "lon", -hop) for hop in range(2, hops + 1)]

    basis_values = basis_table(quad_weights, cycle_index, widths, count)
    near_sources = flat_sources(
        basis_values[:, :, :, reach - NEAR : reach + NEAR + 1], columns + 2 * NEAR, 256)
    polar_values = lax.dynamic_slice_in_dim(basis_values, start, POLAR, 0)
    wide_sources = flat_sources(polar_values, columns + 2 * reach, 512)

    def edge(row):
        return jnp.concatenate(
            [from_west[row * NEAR : (row + 1) * NEAR][None], features[row : row + 1],
             from_east[row * NEAR : (row + 1) * NEAR][None]], axis=1)

    count_lat = lax.axis_size("lat")
    up = [(i, i + 1) for i in range(count_lat - 1)]
    down = [(j, i) for i, j in up]
    north = lax.ppermute(edge(lat_rows - 1), "lat", up)
    south = lax.ppermute(edge(0), "lat", down)
    out = near_call(scalars, near_sources, features, from_west, from_east, north, south,
                    mix_weight)

    west_one = from_west[near_count:].reshape(window.shape)
    east_one = from_east[near_count:].reshape(window.shape)
    wide = jnp.concatenate(west_far + [west_one, window, east_one] + east_far, axis=1)
    wide = wide[:, hops * columns - reach : hops * columns + columns + reach]
    wide = jnp.pad(wide, ((0, 1), (0, 0), (0, 0)))
    return wide_call(scalars, wide, wide_sources, features, mix_weight, out)


def solution(mesh):
    in_specs = (P("lat", "lon", None), P("lat", None, None), P("lat", None, None), P("lat"), P())
    out_specs = P("lat", "lon", None)
    return jax.shard_map(body, mesh=mesh, in_specs=in_specs, out_specs=out_specs, check_vma=False)
```

```python
import functools

import jax
import jax.numpy as jnp
from jax import lax
from jax.experimental import pallas as pl
from jax.experimental.pallas import tpu as pltpu
from jax.sharding import PartitionSpec as P

POLAR = 8
NEAR = 16
BLOCK = 8
NEAR_BLOCK = 32


def shifted(block, axis, distance):
    devices = range(lax.axis_size(axis))
    route = [((i - distance) % len(devices), i) for i in devices]
    return lax.ppermute(block, axis, route)


def lat_extended(value):
    count, length = lax.axis_size("lat"), value.shape[0]
    up = [(i, i + 1) for i in range(count - 1)]
    down = [(j, i) for i, j in up]
    before = lax.ppermute(value[length - 1 :], "lat", up)
    after = lax.ppermute(value[:1], "lat", down)
    return jnp.concatenate([before, value, after], axis=0)


def basis_table(quad_weights, cycle_index, widths, count):
    offsets = jnp.arange(quad_weights.shape[2]) - quad_weights.shape[2] // 2
    inside = jnp.abs(offsets)[None, None, :] <= widths[:, None, None]
    member = cycle_index[:, None, :, :] == jnp.arange(count)[None, :, None, None]
    scale_row = 1.0 / jnp.sqrt(3.0 * (2.0 * widths.astype(jnp.float32) + 1.0))
    values = jnp.where(
        member & inside[:, None, :, :], quad_weights[:, None, :, :], jnp.float32(0.0)
    )
    return (values * scale_row[:, None, None, None]).astype(jnp.bfloat16)


def flat_sources(values, span, lanes):
    rows, count, offsets, taps = values.shape
    flat = jnp.pad(values, ((0, 0), (0, 0), (0, 0), (0, span - taps)))
    flat = flat.reshape(rows, count, offsets * span)
    return jnp.pad(flat, ((0, 0), (0, 0), (0, lanes - offsets * span)))


def conv_block(ext_ref, src_ref, f_ref, w_ref, o_ref, conv_scr, base):
    rows, columns, channels = f_ref.shape
    count, lanes = src_ref.shape[1], src_ref.shape[2]
    span = ext_ref.shape[1]
    for q in range(rows):
        source = src_ref[q].astype(jnp.float32)
        pieces = []
        for b in range(count):
            spread = jnp.broadcast_to(source[b : b + 1], (columns, lanes))
            pieces.append(pltpu.roll(spread, 0, 1, stride=1, stride_axis=0))
        kernel = jnp.concatenate(pieces, axis=0).astype(jnp.bfloat16)
        window = ext_ref[pl.ds(base + q, 4)].reshape(4 * span, channels)[:lanes]
        conv = jnp.dot(kernel, window, preferred_element_type=jnp.float32)
        conv = conv.astype(jnp.bfloat16)
        for b in range(count):
            conv_scr[b, q * columns : (q + 1) * columns, :] = conv[b * columns : (b + 1) * columns]
    acc = f_ref[...].reshape(rows * columns, channels).astype(jnp.float32)
    for b in range(count):
        acc = acc + jnp.dot(conv_scr[b], w_ref[b], preferred_element_type=jnp.float32)
    o_ref[...] = acc.reshape(rows, columns, channels).astype(o_ref.dtype)


def near_kernel(scalar_ref, src_ref, f_ref, all_ref, west_ref, east_ref, north_ref,
                south_ref, w_ref, o_ref, ext_scr, conv_scr):
    rows, columns, channels = f_ref.shape
    lat_rows = all_ref.shape[0]
    halo = (ext_scr.shape[1] - columns) // 2
    step = pl.program_id(0)
    base = step * rows

    def put(k, row):
        ext_scr[k, :halo] = west_ref[pl.ds(pl.multiple_of(row * halo, halo), halo)]
        ext_scr[k, halo : halo + columns] = all_ref[row]
        ext_scr[k, halo + columns :] = east_ref[pl.ds(pl.multiple_of(row * halo, halo), halo)]

    for k in range(1, rows + 1):
        put(k, base + k - 1)

    @pl.when(step == 0)
    def _():
        ext_scr[0] = north_ref[0]

    @pl.when(step > 0)
    def _():
        put(0, base - 1)

    @pl.when(step == pl.num_programs(0) - 1)
    def _():
        ext_scr[rows + 1] = south_ref[0]

    @pl.when(step < pl.num_programs(0) - 1)
    def _():
        put(rows + 1, jnp.minimum(base + rows, lat_rows - 1))

    ext_scr[rows + 2] = jnp.zeros(ext_scr.shape[1:], ext_scr.dtype)
    conv_block(ext_scr, src_ref, f_ref, w_ref, o_ref, conv_scr, 0)


def wide_kernel(scalar_ref, ext_ref, src_ref, f_ref, w_ref, prev_ref, o_ref, conv_scr):
    @pl.when(scalar_ref[1] != 0)
    def _():
        conv_block(ext_ref, src_ref, f_ref, w_ref, o_ref, conv_scr, 0)

    @pl.when(scalar_ref[1] == 0)
    def _():
        o_ref[...] = prev_ref[...]


def full_spec(shape):
    return pl.BlockSpec(shape, lambda i, s: (0,) * len(shape))


def near_call(scalars, sources, features, west, east, north, south, mix_weight):
    lat_rows, columns, channels = features.shape
    count = mix_weight.shape[0]
    halo = (north.shape[1] - columns) // 2
    row_map = lambda i, s: (i, 0, 0)
    grid_spec = pltpu.PrefetchScalarGridSpec(
        num_scalar_prefetch=1,
        grid=(lat_rows // NEAR_BLOCK,),
        in_specs=[
            pl.BlockSpec((NEAR_BLOCK,) + sources.shape[1:], row_map),
            pl.BlockSpec((NEAR_BLOCK, columns, channels), row_map),
            full_spec(features.shape), full_spec(west.shape), full_spec(east.shape),
            full_spec(north.shape), full_spec(south.shape), full_spec(mix_weight.shape),
        ],
        out_specs=pl.BlockSpec((NEAR_BLOCK, columns, channels), row_map),
        scratch_shapes=[
            pltpu.VMEM((NEAR_BLOCK + 3, columns + 2 * halo, channels), features.dtype),
            pltpu.VMEM((count, NEAR_BLOCK * columns, channels), jnp.bfloat16),
        ],
    )
    return pl.pallas_call(
        near_kernel, grid_spec=grid_spec,
        out_shape=jax.ShapeDtypeStruct(features.shape, features.dtype),
    )(scalars, sources, features, features, west, east, north, south, mix_weight)


def wide_call(scalars, extended, sources, features, mix_weight, previous):
    lat_rows, columns, channels = features.shape
    count = mix_weight.shape[0]
    row_map = lambda i, s: (s[0] // BLOCK + i, 0, 0)
    grid_spec = pltpu.PrefetchScalarGridSpec(
        num_scalar_prefetch=1,
        grid=(sources.shape[0] // BLOCK,),
        in_specs=[
            full_spec(extended.shape),
            pl.BlockSpec((BLOCK,) + sources.shape[1:], lambda i, s: (i, 0, 0)),
            pl.BlockSpec((BLOCK, columns, channels), row_map),
            full_spec(mix_weight.shape),
            pl.BlockSpec((BLOCK, columns, channels), row_map),
        ],
        out_specs=pl.BlockSpec((BLOCK, columns, channels), row_map),
        scratch_shapes=[pltpu.VMEM((count, BLOCK * columns, channels), jnp.bfloat16)],
    )
    return pl.pallas_call(
        wide_kernel, grid_spec=grid_spec,
        out_shape=jax.ShapeDtypeStruct(features.shape, features.dtype),
        input_output_aliases={5: 0},
    )(scalars, extended, sources, features, mix_weight, previous)


def body(features, quad_weights, cycle_index, widths, mix_weight):
    count = mix_weight.shape[0]
    lat_rows, columns, channels = features.shape
    reach = quad_weights.shape[2] // 2
    hops = reach // columns

    lat_index, lat_count = lax.axis_index("lat"), lax.axis_size("lat")
    last_band = lat_index == lat_count - 1
    polar = (lat_index == 0) | last_band
    start = jnp.where(last_band, lat_rows - POLAR, 0).astype(jnp.int32)
    scalars = jnp.stack([start, polar.astype(jnp.int32)])

    zero_row = jnp.zeros((1, columns, channels), features.dtype)
    window = lax.dynamic_slice_in_dim(
        jnp.concatenate([zero_row, features, zero_row], axis=0), start, POLAR + 2, 0)
    flat_window = window.reshape(-1, channels)
    near_count = lat_rows * NEAR
    from_west = shifted(jnp.concatenate(
        [features[:, columns - NEAR :].reshape(-1, channels), flat_window]), "lon", 1)
    from_east = shifted(jnp.concatenate(
        [features[:, :NEAR].reshape(-1, channels), flat_window]), "lon", -1)
    late_window, from_west, from_east = lax.optimization_barrier((window, from_west, from_east))
    west_far = [shifted(late_window, "lon", hop) for hop in range(hops, 1, -1)]
    east_far = [shifted(late_window, "lon", -hop) for hop in range(2, hops + 1)]

    basis_values = basis_table(quad_weights, cycle_index, widths, count)
    near_sources = flat_sources(
        basis_values[:, :, :, reach - NEAR : reach + NEAR + 1], columns + 2 * NEAR, 256)
    polar_values = lax.dynamic_slice_in_dim(basis_values, start, POLAR, 0)
    wide_sources = flat_sources(polar_values, columns + 2 * reach, 512)

    def edge(row):
        return jnp.concatenate(
            [from_west[row * NEAR : (row + 1) * NEAR][None], features[row : row + 1],
             from_east[row * NEAR : (row + 1) * NEAR][None]], axis=1)

    count_lat = lax.axis_size("lat")
    up = [(i, i + 1) for i in range(count_lat - 1)]
    down = [(j, i) for i, j in up]
    north = lax.ppermute(edge(lat_rows - 1), "lat", up)
    south = lax.ppermute(edge(0), "lat", down)
    out = near_call(scalars, near_sources, features, from_west, from_east, north, south,
                    mix_weight)

    west_one = from_west[near_count:].reshape(window.shape)
    east_one = from_east[near_count:].reshape(window.shape)
    wide = jnp.concatenate(west_far + [west_one, window, east_one] + east_far, axis=1)
    wide = wide[:, hops * columns - reach : hops * columns + columns + reach]
    wide = jnp.pad(wide, ((0, 1), (0, 0), (0, 0)))
    return wide_call(scalars, wide, wide_sources, features, mix_weight, out)


def solution(mesh):
    in_specs = (P("lat", "lon", None), P("lat", None, None), P("lat", None, None), P("lat"), P())
    out_specs = P("lat", "lon", None)
    return jax.shard_map(body, mesh=mesh, in_specs=in_specs, out_specs=out_specs, check_vma=False)
```

```python
import functools

import jax
import jax.numpy as jnp
from jax import lax
from jax.experimental import pallas as pl
from jax.experimental.pallas import tpu as pltpu
from jax.sharding import PartitionSpec as P

POLAR = 8
NEAR = 16
BLOCK = 8
NEAR_BLOCK = 32


def shifted(block, axis, distance):
    devices = range(lax.axis_size(axis))
    route = [((i - distance) % len(devices), i) for i in devices]
    return lax.ppermute(block, axis, route)


def lat_extended(value):
    count, length = lax.axis_size("lat"), value.shape[0]
    up = [(i, i + 1) for i in range(count - 1)]
    down = [(j, i) for i, j in up]
    before = lax.ppermute(value[length - 1 :], "lat", up)
    after = lax.ppermute(value[:1], "lat", down)
    return jnp.concatenate([before, value, after], axis=0)


def basis_table(quad_weights, cycle_index, widths, count):
    offsets = jnp.arange(quad_weights.shape[2]) - quad_weights.shape[2] // 2
    inside = jnp.abs(offsets)[None, None, :] <= widths[:, None, None]
    member = cycle_index[:, None, :, :] == jnp.arange(count)[None, :, None, None]
    scale_row = 1.0 / jnp.sqrt(3.0 * (2.0 * widths.astype(jnp.float32) + 1.0))
    values = jnp.where(
        member & inside[:, None, :, :], quad_weights[:, None, :, :], jnp.float32(0.0)
    )
    return (values * scale_row[:, None, None, None]).astype(jnp.bfloat16)


def flat_sources(values, span, lanes):
    rows, count, offsets, taps = values.shape
    flat = jnp.pad(values, ((0, 0), (0, 0), (0, 0), (0, span - taps)))
    flat = flat.reshape(rows, count, offsets * span)
    return jnp.pad(flat, ((0, 0), (0, 0), (0, lanes - offsets * span)))


def conv_block(ext_ref, src_ref, f_ref, w_ref, o_ref, conv_scr, base):
    rows, columns, channels = f_ref.shape
    count, lanes = src_ref.shape[1], src_ref.shape[2]
    span = ext_ref.shape[1]
    for q in range(rows):
        source = src_ref[q].astype(jnp.float32)
        pieces = []
        for b in range(count):
            spread = jnp.broadcast_to(source[b : b + 1], (columns, lanes))
            pieces.append(pltpu.roll(spread, 0, 1, stride=1, stride_axis=0))
        kernel = jnp.concatenate(pieces, axis=0).astype(jnp.bfloat16)
        window = ext_ref[pl.ds(base + q, 4)].reshape(4 * span, channels)[:lanes]
        conv = jnp.dot(kernel, window, preferred_element_type=jnp.float32)
        conv = conv.astype(jnp.bfloat16)
        for b in range(count):
            conv_scr[b, q * columns : (q + 1) * columns, :] = conv[b * columns : (b + 1) * columns]
    acc = f_ref[...].reshape(rows * columns, channels).astype(jnp.float32)
    for b in range(count):
        acc = acc + jnp.dot(conv_scr[b], w_ref[b], preferred_element_type=jnp.float32)
    o_ref[...] = acc.reshape(rows, columns, channels).astype(o_ref.dtype)


def near_kernel(scalar_ref, src_ref, f_ref, all_ref, west_ref, east_ref, north_ref,
                south_ref, w_ref, o_ref, ext_scr, conv_scr):
    rows, columns, channels = f_ref.shape
    lat_rows = all_ref.shape[0]
    halo = (ext_scr.shape[1] - columns) // 2
    step = pl.program_id(0)
    base = step * rows

    def put(k, row):
        ext_scr[k, :halo] = west_ref[pl.ds(pl.multiple_of(row * halo, halo), halo)]
        ext_scr[k, halo : halo + columns] = all_ref[row]
        ext_scr[k, halo + columns :] = east_ref[pl.ds(pl.multiple_of(row * halo, halo), halo)]

    for k in range(1, rows + 1):
        put(k, base + k - 1)

    @pl.when(step == 0)
    def _():
        ext_scr[0] = north_ref[0]

    @pl.when(step > 0)
    def _():
        put(0, base - 1)

    @pl.when(step == pl.num_programs(0) - 1)
    def _():
        ext_scr[rows + 1] = south_ref[0]

    @pl.when(step < pl.num_programs(0) - 1)
    def _():
        put(rows + 1, jnp.minimum(base + rows, lat_rows - 1))

    ext_scr[rows + 2] = jnp.zeros(ext_scr.shape[1:], ext_scr.dtype)
    conv_block(ext_scr, src_ref, f_ref, w_ref, o_ref, conv_scr, 0)


def wide_kernel(scalar_ref, ext_ref, src_ref, f_ref, w_ref, prev_ref, o_ref, conv_scr):
    @pl.when(scalar_ref[1] != 0)
    def _():
        conv_block(ext_ref, src_ref, f_ref, w_ref, o_ref, conv_scr, 0)

    @pl.when(scalar_ref[1] == 0)
    def _():
        o_ref[...] = prev_ref[...]


def full_spec(shape):
    return pl.BlockSpec(shape, lambda i, s: (0,) * len(shape))


def near_call(scalars, sources, features, west, east, north, south, mix_weight):
    lat_rows, columns, channels = features.shape
    count = mix_weight.shape[0]
    halo = (north.shape[1] - columns) // 2
    row_map = lambda i, s: (i, 0, 0)
    grid_spec = pltpu.PrefetchScalarGridSpec(
        num_scalar_prefetch=1,
        grid=(lat_rows // NEAR_BLOCK,),
        in_specs=[
            pl.BlockSpec((NEAR_BLOCK,) + sources.shape[1:], row_map),
            pl.BlockSpec((NEAR_BLOCK, columns, channels), row_map),
            full_spec(features.shape), full_spec(west.shape), full_spec(east.shape),
            full_spec(north.shape), full_spec(south.shape), full_spec(mix_weight.shape),
        ],
        out_specs=pl.BlockSpec((NEAR_BLOCK, columns, channels), row_map),
        scratch_shapes=[
            pltpu.VMEM((NEAR_BLOCK + 3, columns + 2 * halo, channels), features.dtype),
            pltpu.VMEM((count, NEAR_BLOCK * columns, channels), jnp.bfloat16),
        ],
    )
    return pl.pallas_call(
        near_kernel, grid_spec=grid_spec,
        out_shape=jax.ShapeDtypeStruct(features.shape, features.dtype),
    )(scalars, sources, features, features, west, east, north, south, mix_weight)


def wide_call(scalars, extended, sources, features, mix_weight, previous):
    lat_rows, columns, channels = features.shape
    count = mix_weight.shape[0]
    row_map = lambda i, s: (s[0] // BLOCK + i, 0, 0)
    grid_spec = pltpu.PrefetchScalarGridSpec(
        num_scalar_prefetch=1,
        grid=(sources.shape[0] // BLOCK,),
        in_specs=[
            full_spec(extended.shape),
            pl.BlockSpec((BLOCK,) + sources.shape[1:], lambda i, s: (i, 0, 0)),
            pl.BlockSpec((BLOCK, columns, channels), row_map),
            full_spec(mix_weight.shape),
            pl.BlockSpec((BLOCK, columns, channels), row_map),
        ],
        out_specs=pl.BlockSpec((BLOCK, columns, channels), row_map),
        scratch_shapes=[pltpu.VMEM((count, BLOCK * columns, channels), jnp.bfloat16)],
    )
    return pl.pallas_call(
        wide_kernel, grid_spec=grid_spec,
        out_shape=jax.ShapeDtypeStruct(features.shape, features.dtype),
        input_output_aliases={5: 0},
    )(scalars, extended, sources, features, mix_weight, previous)


def body(features, quad_weights, cycle_index, widths, mix_weight):
    count = mix_weight.shape[0]
    lat_rows, columns, channels = features.shape
    reach = quad_weights.shape[2] // 2
    hops = reach // columns

    lat_index, lat_count = lax.axis_index("lat"), lax.axis_size("lat")
    last_band = lat_index == lat_count - 1
    polar = (lat_index == 0) | last_band
    start = jnp.where(last_band, lat_rows - POLAR, 0).astype(jnp.int32)
    scalars = jnp.stack([start, polar.astype(jnp.int32)])

    zero_row = jnp.zeros((1, columns, channels), features.dtype)
    window = lax.dynamic_slice_in_dim(
        jnp.concatenate([zero_row, features, zero_row], axis=0), start, POLAR + 2, 0)
    flat_window = window.reshape(-1, channels)
    near_count = lat_rows * NEAR
    from_west = shifted(jnp.concatenate(
        [features[:, columns - NEAR :].reshape(-1, channels), flat_window]), "lon", 1)
    from_east = shifted(jnp.concatenate(
        [features[:, :NEAR].reshape(-1, channels), flat_window]), "lon", -1)
    west_far = [shifted(window, "lon", hop) for hop in range(hops, 1, -1)]
    east_far = [shifted(window, "lon", -hop) for hop in range(2, hops + 1)]

    basis_values = basis_table(quad_weights, cycle_index, widths, count)
    near_sources = flat_sources(
        basis_values[:, :, :, reach - NEAR : reach + NEAR + 1], columns + 2 * NEAR, 256)
    polar_values = lax.dynamic_slice_in_dim(basis_values, start, POLAR, 0)
    wide_sources = flat_sources(polar_values, columns + 2 * reach, 512)

    lon_count = lax.axis_size("lon")

    def from_band(block, lat_step, lon_step):
        pairs = []
        for a in range(count_lat):
            if 0 <= a - lat_step < count_lat:
                for b in range(lon_count):
                    source = (a - lat_step) * lon_count + (b - lon_step) % lon_count
                    pairs.append((source, a * lon_count + b))
        return lax.ppermute(block, ("lat", "lon"), pairs)

    count_lat = lax.axis_size("lat")
    last, first = features[lat_rows - 1 :], features[:1]
    north = jnp.concatenate(
        [from_band(last[:, columns - NEAR :], 1, 1), from_band(last, 1, 0),
         from_band(last[:, :NEAR], 1, -1)], axis=1)
    south = jnp.concatenate(
        [from_band(first[:, columns - NEAR :], -1, 1), from_band(first, -1, 0),
         from_band(first[:, :NEAR], -1, -1)], axis=1)
    out = near_call(scalars, near_sources, features, from_west, from_east, north, south,
                    mix_weight)

    west_one = from_west[near_count:].reshape(window.shape)
    east_one = from_east[near_count:].reshape(window.shape)
    wide = jnp.concatenate(west_far + [west_one, window, east_one] + east_far, axis=1)
    wide = wide[:, hops * columns - reach : hops * columns + columns + reach]
    wide = jnp.pad(wide, ((0, 1), (0, 0), (0, 0)))
    return wide_call(scalars, wide, wide_sources, features, mix_weight, out)


def solution(mesh):
    in_specs = (P("lat", "lon", None), P("lat", None, None), P("lat", None, None), P("lat"), P())
    out_specs = P("lat", "lon", None)
    return jax.shard_map(body, mesh=mesh, in_specs=in_specs, out_specs=out_specs, check_vma=False)
```

```python
import functools

import jax
import jax.numpy as jnp
from jax import lax
from jax.experimental import pallas as pl
from jax.experimental.pallas import tpu as pltpu
from jax.sharding import PartitionSpec as P

POLAR = 8
NEAR = 16
BLOCK = 8
NEAR_BLOCK = 16


def shifted(block, axis, distance):
    devices = range(lax.axis_size(axis))
    route = [((i - distance) % len(devices), i) for i in devices]
    return lax.ppermute(block, axis, route)


def lat_extended(value):
    count, length = lax.axis_size("lat"), value.shape[0]
    up = [(i, i + 1) for i in range(count - 1)]
    down = [(j, i) for i, j in up]
    before = lax.ppermute(value[length - 1 :], "lat", up)
    after = lax.ppermute(value[:1], "lat", down)
    return jnp.concatenate([before, value, after], axis=0)


def basis_table(quad_weights, cycle_index, widths, count):
    offsets = jnp.arange(quad_weights.shape[2]) - quad_weights.shape[2] // 2
    inside = jnp.abs(offsets)[None, None, :] <= widths[:, None, None]
    member = cycle_index[:, None, :, :] == jnp.arange(count)[None, :, None, None]
    scale_row = 1.0 / jnp.sqrt(3.0 * (2.0 * widths.astype(jnp.float32) + 1.0))
    values = jnp.where(
        member & inside[:, None, :, :], quad_weights[:, None, :, :], jnp.float32(0.0)
    )
    return (values * scale_row[:, None, None, None]).astype(jnp.bfloat16)


def flat_sources(values, span, lanes):
    rows, count, offsets, taps = values.shape
    flat = jnp.pad(values, ((0, 0), (0, 0), (0, 0), (0, span - taps)))
    flat = flat.reshape(rows, count, offsets * span)
    return jnp.pad(flat, ((0, 0), (0, 0), (0, lanes - offsets * span)))


def conv_block(ext_ref, src_ref, f_ref, w_ref, o_ref, conv_scr, base):
    rows, columns, channels = f_ref.shape
    count, lanes = src_ref.shape[1], src_ref.shape[2]
    span = ext_ref.shape[1]
    for q in range(rows):
        source = src_ref[q].astype(jnp.float32)
        pieces = []
        for b in range(count):
            spread = jnp.broadcast_to(source[b : b + 1], (columns, lanes))
            pieces.append(pltpu.roll(spread, 0, 1, stride=1, stride_axis=0))
        kernel = jnp.concatenate(pieces, axis=0).astype(jnp.bfloat16)
        window = ext_ref[pl.ds(base + q, 4)].reshape(4 * span, channels)[:lanes]
        conv = jnp.dot(kernel, window, preferred_element_type=jnp.float32)
        conv = conv.astype(jnp.bfloat16)
        for b in range(count):
            conv_scr[b, q * columns : (q + 1) * columns, :] = conv[b * columns : (b + 1) * columns]
    acc = f_ref[...].reshape(rows * columns, channels).astype(jnp.float32)
    for b in range(count):
        acc = acc + jnp.dot(conv_scr[b], w_ref[b], preferred_element_type=jnp.float32)
    o_ref[...] = acc.reshape(rows, columns, channels).astype(o_ref.dtype)


def near_kernel(scalar_ref, src_ref, f_ref, all_ref, west_ref, east_ref, north_ref,
                south_ref, w_ref, *rest, first, lowest):
    o_ref, ext_scr, conv_scr = rest[-3], rest[-2], rest[-1]
    rows, columns, channels = f_ref.shape
    lat_rows = all_ref.shape[0]
    halo = (ext_scr.shape[1] - columns) // 2
    step = pl.program_id(0)
    base = first + step * rows

    def sides(k, row):
        start = pl.multiple_of((row - lowest) * halo, halo)
        ext_scr[k, :halo] = west_ref[pl.ds(start, halo)]
        ext_scr[k, halo + columns :] = east_ref[pl.ds(start, halo)]

    for k in range(rows + 2):
        sides(k, base + k - 1)
    for k in range(1, rows + 1):
        ext_scr[k, halo : halo + columns] = all_ref[base + k - 1]

    @pl.when(base == 0)
    def _():
        ext_scr[0, halo : halo + columns] = north_ref[0]

    @pl.when(base > 0)
    def _():
        ext_scr[0, halo : halo + columns] = all_ref[jnp.maximum(base - 1, 0)]

    @pl.when(base + rows == lat_rows)
    def _():
        ext_scr[rows + 1, halo : halo + columns] = south_ref[0]

    @pl.when(base + rows < lat_rows)
    def _():
        ext_scr[rows + 1, halo : halo + columns] = all_ref[jnp.minimum(base + rows, lat_rows - 1)]

    ext_scr[rows + 2] = jnp.zeros(ext_scr.shape[1:], ext_scr.dtype)
    conv_block(ext_scr, src_ref, f_ref, w_ref, o_ref, conv_scr, 0)


def wide_kernel(scalar_ref, ext_ref, src_ref, f_ref, w_ref, prev_ref, o_ref, conv_scr):
    @pl.when(scalar_ref[1] != 0)
    def _():
        conv_block(ext_ref, src_ref, f_ref, w_ref, o_ref, conv_scr, 0)

    @pl.when(scalar_ref[1] == 0)
    def _():
        o_ref[...] = prev_ref[...]


def full_spec(shape):
    return pl.BlockSpec(shape, lambda i, s: (0,) * len(shape))


def near_call(scalars, sources, features, west, east, north, south, mix_weight,
              first, count_rows, lowest, previous=None):
    lat_rows, columns, channels = features.shape
    count = mix_weight.shape[0]
    halo = NEAR
    offset = first // NEAR_BLOCK
    row_map = lambda i, s: (i + offset, 0, 0)
    in_specs = [
        pl.BlockSpec((NEAR_BLOCK,) + sources.shape[1:], row_map),
        pl.BlockSpec((NEAR_BLOCK, columns, channels), row_map),
        full_spec(features.shape), full_spec(west.shape), full_spec(east.shape),
        full_spec(north.shape), full_spec(south.shape), full_spec(mix_weight.shape),
    ]
    operands = [scalars, sources, features, features, west, east, north, south, mix_weight]
    aliases = {}
    if previous is not None:
        in_specs.append(pl.BlockSpec(memory_space=pl.ANY))
        operands.append(previous)
        aliases = {len(operands) - 1: 0}
    grid_spec = pltpu.PrefetchScalarGridSpec(
        num_scalar_prefetch=1,
        grid=(count_rows // NEAR_BLOCK,),
        in_specs=in_specs,
        out_specs=pl.BlockSpec((NEAR_BLOCK, columns, channels), row_map),
        scratch_shapes=[
            pltpu.VMEM((NEAR_BLOCK + 3, columns + 2 * halo, channels), features.dtype),
            pltpu.VMEM((count, NEAR_BLOCK * columns, channels), jnp.bfloat16),
        ],
    )
    return pl.pallas_call(
        functools.partial(near_kernel, first=first, lowest=lowest), grid_spec=grid_spec,
        out_shape=jax.ShapeDtypeStruct(features.shape, features.dtype),
        input_output_aliases=aliases,
    )(*operands)


def wide_call(scalars, extended, sources, features, mix_weight, previous):
    lat_rows, columns, channels = features.shape
    count = mix_weight.shape[0]
    row_map = lambda i, s: (s[0] // BLOCK + i, 0, 0)
    grid_spec = pltpu.PrefetchScalarGridSpec(
        num_scalar_prefetch=1,
        grid=(sources.shape[0] // BLOCK,),
        in_specs=[
            full_spec(extended.shape),
            pl.BlockSpec((BLOCK,) + sources.shape[1:], lambda i, s: (i, 0, 0)),
            pl.BlockSpec((BLOCK, columns, channels), row_map),
            full_spec(mix_weight.shape),
            pl.BlockSpec((BLOCK, columns, channels), row_map),
        ],
        out_specs=pl.BlockSpec((BLOCK, columns, channels), row_map),
        scratch_shapes=[pltpu.VMEM((count, BLOCK * columns, channels), jnp.bfloat16)],
    )
    return pl.pallas_call(
        wide_kernel, grid_spec=grid_spec,
        out_shape=jax.ShapeDtypeStruct(features.shape, features.dtype),
        input_output_aliases={5: 0},
    )(scalars, extended, sources, features, mix_weight, previous)


def body(features, quad_weights, cycle_index, widths, mix_weight):
    count = mix_weight.shape[0]
    lat_rows, columns, channels = features.shape
    reach = quad_weights.shape[2] // 2
    hops = reach // columns

    lat_index, lat_count = lax.axis_index("lat"), lax.axis_size("lat")
    last_band = lat_index == lat_count - 1
    polar = (lat_index == 0) | last_band
    start = jnp.where(last_band, lat_rows - POLAR, 0).astype(jnp.int32)
    scalars = jnp.stack([start, polar.astype(jnp.int32)])

    zero_row = jnp.zeros((1, columns, channels), features.dtype)
    window = lax.dynamic_slice_in_dim(
        jnp.concatenate([zero_row, features, zero_row], axis=0), start, POLAR + 2, 0)
    flat_window = window.reshape(-1, channels)
    count_lat = lax.axis_size("lat")
    up = [(i, i + 1) for i in range(count_lat - 1)]
    down = [(j, i) for i, j in up]
    north = lax.ppermute(features[lat_rows - 1 :], "lat", up)
    south = lax.ppermute(features[:1], "lat", down)
    padded = jnp.concatenate([north, features, south], axis=0)
    half = lat_rows // 2
    head = padded[: half + 2]
    tail = padded[half:]
    head_west = shifted(head[:, columns - NEAR :].reshape(-1, channels), "lon", 1)
    head_east = shifted(head[:, :NEAR].reshape(-1, channels), "lon", -1)
    from_west = shifted(jnp.concatenate(
        [tail[:, columns - NEAR :].reshape(-1, channels), flat_window]), "lon", 1)
    from_east = shifted(jnp.concatenate(
        [tail[:, :NEAR].reshape(-1, channels), flat_window]), "lon", -1)
    near_count = tail.shape[0] * NEAR
    west_far = [shifted(window, "lon", hop) for hop in range(hops, 1, -1)]
    east_far = [shifted(window, "lon", -hop) for hop in range(2, hops + 1)]

    basis_values = basis_table(quad_weights, cycle_index, widths, count)
    near_sources = flat_sources(
        basis_values[:, :, :, reach - NEAR : reach + NEAR + 1], columns + 2 * NEAR, 256)
    polar_values = lax.dynamic_slice_in_dim(basis_values, start, POLAR, 0)
    wide_sources = flat_sources(polar_values, columns + 2 * reach, 512)

    out = near_call(scalars, near_sources, features, head_west, head_east, north, south,
                    mix_weight, 0, half, -1)
    out = near_call(scalars, near_sources, features, from_west, from_east, north, south,
                    mix_weight, half, lat_rows - half, half - 1, previous=out)

    west_one = from_west[near_count:].reshape(window.shape)
    east_one = from_east[near_count:].reshape(window.shape)
    wide = jnp.concatenate(west_far + [west_one, window, east_one] + east_far, axis=1)
    wide = wide[:, hops * columns - reach : hops * columns + columns + reach]
    wide = jnp.pad(wide, ((0, 1), (0, 0), (0, 0)))
    return wide_call(scalars, wide, wide_sources, features, mix_weight, out)


def solution(mesh):
    in_specs = (P("lat", "lon", None), P("lat", None, None), P("lat", None, None), P("lat"), P())
    out_specs = P("lat", "lon", None)
    return jax.shard_map(body, mesh=mesh, in_specs=in_specs, out_specs=out_specs, check_vma=False)
```

```python
import functools

import jax
import jax.numpy as jnp
from jax import lax
from jax.experimental import pallas as pl
from jax.experimental.pallas import tpu as pltpu
from jax.sharding import PartitionSpec as P

POLAR = 8
NEAR = 16
BLOCK = 8
NEAR_BLOCK = 24


def shifted(block, axis, distance):
    devices = range(lax.axis_size(axis))
    route = [((i - distance) % len(devices), i) for i in devices]
    return lax.ppermute(block, axis, route)


def lat_extended(value):
    count, length = lax.axis_size("lat"), value.shape[0]
    up = [(i, i + 1) for i in range(count - 1)]
    down = [(j, i) for i, j in up]
    before = lax.ppermute(value[length - 1 :], "lat", up)
    after = lax.ppermute(value[:1], "lat", down)
    return jnp.concatenate([before, value, after], axis=0)


def basis_table(quad_weights, cycle_index, widths, count):
    offsets = jnp.arange(quad_weights.shape[2]) - quad_weights.shape[2] // 2
    inside = jnp.abs(offsets)[None, None, :] <= widths[:, None, None]
    member = cycle_index[:, None, :, :] == jnp.arange(count)[None, :, None, None]
    scale_row = 1.0 / jnp.sqrt(3.0 * (2.0 * widths.astype(jnp.float32) + 1.0))
    values = jnp.where(
        member & inside[:, None, :, :], quad_weights[:, None, :, :], jnp.float32(0.0)
    )
    return (values * scale_row[:, None, None, None]).astype(jnp.bfloat16)


def flat_sources(values, span, lanes):
    rows, count, offsets, taps = values.shape
    flat = jnp.pad(values, ((0, 0), (0, 0), (0, 0), (0, span - taps)))
    flat = flat.reshape(rows, count, offsets * span)
    return jnp.pad(flat, ((0, 0), (0, 0), (0, lanes - offsets * span)))


def conv_block(ext_ref, src_ref, f_ref, w_ref, o_ref, conv_scr, base):
    rows, columns, channels = f_ref.shape
    count, lanes = src_ref.shape[1], src_ref.shape[2]
    span = ext_ref.shape[1]
    for q in range(rows):
        source = src_ref[q].astype(jnp.float32)
        pieces = []
        for b in range(count):
            spread = jnp.broadcast_to(source[b : b + 1], (columns, lanes))
            pieces.append(pltpu.roll(spread, 0, 1, stride=1, stride_axis=0))
        kernel = jnp.concatenate(pieces, axis=0).astype(jnp.bfloat16)
        window = ext_ref[pl.ds(base + q, 4)].reshape(4 * span, channels)[:lanes]
        conv = jnp.dot(kernel, window, preferred_element_type=jnp.float32)
        conv = conv.astype(jnp.bfloat16)
        for b in range(count):
            conv_scr[b, q * columns : (q + 1) * columns, :] = conv[b * columns : (b + 1) * columns]
    acc = f_ref[...].reshape(rows * columns, channels).astype(jnp.float32)
    for b in range(count):
        acc = acc + jnp.dot(conv_scr[b], w_ref[b], preferred_element_type=jnp.float32)
    o_ref[...] = acc.reshape(rows, columns, channels).astype(o_ref.dtype)


def near_kernel(scalar_ref, src_ref, f_ref, all_ref, west_ref, east_ref, north_ref,
                south_ref, w_ref, *rest, first, lowest):
    o_ref, ext_scr, conv_scr = rest[-3], rest[-2], rest[-1]
    rows, columns, channels = f_ref.shape
    lat_rows = all_ref.shape[0]
    halo = (ext_scr.shape[1] - columns) // 2
    step = pl.program_id(0)
    base = first + step * rows

    def sides(k, row):
        start = pl.multiple_of((row - lowest) * halo, halo)
        ext_scr[k, :halo] = west_ref[pl.ds(start, halo)]
        ext_scr[k, halo + columns :] = east_ref[pl.ds(start, halo)]

    for k in range(rows + 2):
        sides(k, base + k - 1)
    for k in range(1, rows + 1):
        ext_scr[k, halo : halo + columns] = all_ref[base + k - 1]

    @pl.when(base == 0)
    def _():
        ext_scr[0, halo : halo + columns] = north_ref[0]

    @pl.when(base > 0)
    def _():
        ext_scr[0, halo : halo + columns] = all_ref[jnp.maximum(base - 1, 0)]

    @pl.when(base + rows == lat_rows)
    def _():
        ext_scr[rows + 1, halo : halo + columns] = south_ref[0]

    @pl.when(base + rows < lat_rows)
    def _():
        ext_scr[rows + 1, halo : halo + columns] = all_ref[jnp.minimum(base + rows, lat_rows - 1)]

    ext_scr[rows + 2] = jnp.zeros(ext_scr.shape[1:], ext_scr.dtype)
    conv_block(ext_scr, src_ref, f_ref, w_ref, o_ref, conv_scr, 0)


def wide_kernel(scalar_ref, ext_ref, src_ref, f_ref, w_ref, prev_ref, o_ref, conv_scr):
    @pl.when(scalar_ref[1] != 0)
    def _():
        conv_block(ext_ref, src_ref, f_ref, w_ref, o_ref, conv_scr, 0)

    @pl.when(scalar_ref[1] == 0)
    def _():
        o_ref[...] = prev_ref[...]


def full_spec(shape):
    return pl.BlockSpec(shape, lambda i, s: (0,) * len(shape))


def near_call(scalars, sources, features, west, east, north, south, mix_weight,
              first, count_rows, lowest, previous=None):
    lat_rows, columns, channels = features.shape
    count = mix_weight.shape[0]
    halo = NEAR
    offset = first // NEAR_BLOCK
    row_map = lambda i, s: (i + offset, 0, 0)
    in_specs = [
        pl.BlockSpec((NEAR_BLOCK,) + sources.shape[1:], row_map),
        pl.BlockSpec((NEAR_BLOCK, columns, channels), row_map),
        full_spec(features.shape), full_spec(west.shape), full_spec(east.shape),
        full_spec(north.shape), full_spec(south.shape), full_spec(mix_weight.shape),
    ]
    operands = [scalars, sources, features, features, west, east, north, south, mix_weight]
    aliases = {}
    if previous is not None:
        in_specs.append(pl.BlockSpec(memory_space=pl.ANY))
        operands.append(previous)
        aliases = {len(operands) - 1: 0}
    grid_spec = pltpu.PrefetchScalarGridSpec(
        num_scalar_prefetch=1,
        grid=(count_rows // NEAR_BLOCK,),
        in_specs=in_specs,
        out_specs=pl.BlockSpec((NEAR_BLOCK, columns, channels), row_map),
        scratch_shapes=[
            pltpu.VMEM((NEAR_BLOCK + 3, columns + 2 * halo, channels), features.dtype),
            pltpu.VMEM((count, NEAR_BLOCK * columns, channels), jnp.bfloat16),
        ],
    )
    return pl.pallas_call(
        functools.partial(near_kernel, first=first, lowest=lowest), grid_spec=grid_spec,
        out_shape=jax.ShapeDtypeStruct(features.shape, features.dtype),
        input_output_aliases=aliases,
    )(*operands)


def wide_call(scalars, extended, sources, features, mix_weight, previous):
    lat_rows, columns, channels = features.shape
    count = mix_weight.shape[0]
    row_map = lambda i, s: (s[0] // BLOCK + i, 0, 0)
    grid_spec = pltpu.PrefetchScalarGridSpec(
        num_scalar_prefetch=1,
        grid=(sources.shape[0] // BLOCK,),
        in_specs=[
            full_spec(extended.shape),
            pl.BlockSpec((BLOCK,) + sources.shape[1:], lambda i, s: (i, 0, 0)),
            pl.BlockSpec((BLOCK, columns, channels), row_map),
            full_spec(mix_weight.shape),
            pl.BlockSpec((BLOCK, columns, channels), row_map),
        ],
        out_specs=pl.BlockSpec((BLOCK, columns, channels), row_map),
        scratch_shapes=[pltpu.VMEM((count, BLOCK * columns, channels), jnp.bfloat16)],
    )
    return pl.pallas_call(
        wide_kernel, grid_spec=grid_spec,
        out_shape=jax.ShapeDtypeStruct(features.shape, features.dtype),
        input_output_aliases={5: 0},
    )(scalars, extended, sources, features, mix_weight, previous)


def body(features, quad_weights, cycle_index, widths, mix_weight):
    count = mix_weight.shape[0]
    lat_rows, columns, channels = features.shape
    reach = quad_weights.shape[2] // 2
    hops = reach // columns

    lat_index, lat_count = lax.axis_index("lat"), lax.axis_size("lat")
    last_band = lat_index == lat_count - 1
    polar = (lat_index == 0) | last_band
    start = jnp.where(last_band, lat_rows - POLAR, 0).astype(jnp.int32)
    scalars = jnp.stack([start, polar.astype(jnp.int32)])

    zero_row = jnp.zeros((1, columns, channels), features.dtype)
    window = lax.dynamic_slice_in_dim(
        jnp.concatenate([zero_row, features, zero_row], axis=0), start, POLAR + 2, 0)
    flat_window = window.reshape(-1, channels)
    count_lat = lax.axis_size("lat")
    up = [(i, i + 1) for i in range(count_lat - 1)]
    down = [(j, i) for i, j in up]
    north = lax.ppermute(features[lat_rows - 1 :], "lat", up)
    south = lax.ppermute(features[:1], "lat", down)
    padded = jnp.concatenate([north, features, south], axis=0)
    half = lat_rows // 2
    head = padded[: half + 2]
    tail = padded[half:]
    head_west = shifted(head[:, columns - NEAR :].reshape(-1, channels), "lon", 1)
    head_east = shifted(head[:, :NEAR].reshape(-1, channels), "lon", -1)
    from_west = shifted(jnp.concatenate(
        [tail[:, columns - NEAR :].reshape(-1, channels), flat_window]), "lon", 1)
    from_east = shifted(jnp.concatenate(
        [tail[:, :NEAR].reshape(-1, channels), flat_window]), "lon", -1)
    near_count = tail.shape[0] * NEAR
    west_far = [shifted(window, "lon", hop) for hop in range(hops, 1, -1)]
    east_far = [shifted(window, "lon", -hop) for hop in range(2, hops + 1)]

    basis_values = basis_table(quad_weights, cycle_index, widths, count)
    near_sources = flat_sources(
        basis_values[:, :, :, reach - NEAR : reach + NEAR + 1], columns + 2 * NEAR, 256)
    polar_values = lax.dynamic_slice_in_dim(basis_values, start, POLAR, 0)
    wide_sources = flat_sources(polar_values, columns + 2 * reach, 512)

    out = near_call(scalars, near_sources, features, head_west, head_east, north, south,
                    mix_weight, 0, half, -1)
    out = near_call(scalars, near_sources, features, from_west, from_east, north, south,
                    mix_weight, half, lat_rows - half, half - 1, previous=out)

    west_one = from_west[near_count:].reshape(window.shape)
    east_one = from_east[near_count:].reshape(window.shape)
    wide = jnp.concatenate(west_far + [west_one, window, east_one] + east_far, axis=1)
    wide = wide[:, hops * columns - reach : hops * columns + columns + reach]
    wide = jnp.pad(wide, ((0, 1), (0, 0), (0, 0)))
    return wide_call(scalars, wide, wide_sources, features, mix_weight, out)


def solution(mesh):
    in_specs = (P("lat", "lon", None), P("lat", None, None), P("lat", None, None), P("lat"), P())
    out_specs = P("lat", "lon", None)
    return jax.shard_map(body, mesh=mesh, in_specs=in_specs, out_specs=out_specs, check_vma=False)
```

```python
import functools

import jax
import jax.numpy as jnp
from jax import lax
from jax.experimental import pallas as pl
from jax.experimental.pallas import tpu as pltpu
from jax.sharding import PartitionSpec as P

POLAR = 8
NEAR = 16
BLOCK = 8
NEAR_BLOCK = 24


def shifted(block, axis, distance):
    devices = range(lax.axis_size(axis))
    route = [((i - distance) % len(devices), i) for i in devices]
    return lax.ppermute(block, axis, route)


def lat_extended(value):
    count, length = lax.axis_size("lat"), value.shape[0]
    up = [(i, i + 1) for i in range(count - 1)]
    down = [(j, i) for i, j in up]
    before = lax.ppermute(value[length - 1 :], "lat", up)
    after = lax.ppermute(value[:1], "lat", down)
    return jnp.concatenate([before, value, after], axis=0)


def basis_table(quad_weights, cycle_index, widths, count):
    offsets = jnp.arange(quad_weights.shape[2]) - quad_weights.shape[2] // 2
    inside = jnp.abs(offsets)[None, None, :] <= widths[:, None, None]
    member = cycle_index[:, None, :, :] == jnp.arange(count)[None, :, None, None]
    scale_row = 1.0 / jnp.sqrt(3.0 * (2.0 * widths.astype(jnp.float32) + 1.0))
    values = jnp.where(
        member & inside[:, None, :, :], quad_weights[:, None, :, :], jnp.float32(0.0)
    )
    return (values * scale_row[:, None, None, None]).astype(jnp.bfloat16)


def flat_sources(values, span, lanes):
    rows, count, offsets, taps = values.shape
    flat = jnp.pad(values, ((0, 0), (0, 0), (0, 0), (0, span - taps)))
    flat = flat.reshape(rows, count, offsets * span)
    return jnp.pad(flat, ((0, 0), (0, 0), (0, lanes - offsets * span)))


def conv_block(ext_ref, src_ref, f_ref, w_ref, o_ref, conv_scr, base, needed=None):
    rows, columns, channels = f_ref.shape
    count, lanes = src_ref.shape[1], src_ref.shape[2]
    span = ext_ref.shape[1]
    for q in range(rows):
        if needed is None:
            conv_row(ext_ref, src_ref, conv_scr, base, q)
        else:
            pl.when(needed(q))(functools.partial(conv_row, ext_ref, src_ref, conv_scr, base, q))
    acc = f_ref[...].reshape(rows * columns, channels).astype(jnp.float32)
    for b in range(count):
        acc = acc + jnp.dot(conv_scr[b], w_ref[b], preferred_element_type=jnp.float32)
    o_ref[...] = acc.reshape(rows, columns, channels).astype(o_ref.dtype)


def conv_row(ext_ref, src_ref, conv_scr, base, q):
    count, lanes = src_ref.shape[1], src_ref.shape[2]
    span, channels = ext_ref.shape[1], ext_ref.shape[2]
    columns = conv_scr.shape[1] // src_ref.shape[0]
    if True:
        source = src_ref[q].astype(jnp.float32)
        pieces = []
        for b in range(count):
            spread = jnp.broadcast_to(source[b : b + 1], (columns, lanes))
            pieces.append(pltpu.roll(spread, 0, 1, stride=1, stride_axis=0))
        kernel = jnp.concatenate(pieces, axis=0).astype(jnp.bfloat16)
        window = ext_ref[pl.ds(base + q, 4)].reshape(4 * span, channels)[:lanes]
        conv = jnp.dot(kernel, window, preferred_element_type=jnp.float32)
        conv = conv.astype(jnp.bfloat16)
        for b in range(count):
            conv_scr[b, q * columns : (q + 1) * columns, :] = conv[b * columns : (b + 1) * columns]


def near_kernel(scalar_ref, src_ref, f_ref, all_ref, west_ref, east_ref, north_ref,
                south_ref, w_ref, *rest, first, lowest):
    o_ref, ext_scr, conv_scr = rest[-3], rest[-2], rest[-1]
    rows, columns, channels = f_ref.shape
    lat_rows = all_ref.shape[0]
    halo = (ext_scr.shape[1] - columns) // 2
    step = pl.program_id(0)
    base = first + step * rows

    def sides(k, row):
        start = pl.multiple_of((row - lowest) * halo, halo)
        ext_scr[k, :halo] = west_ref[pl.ds(start, halo)]
        ext_scr[k, halo + columns :] = east_ref[pl.ds(start, halo)]

    for k in range(rows + 2):
        sides(k, base + k - 1)
    for k in range(1, rows + 1):
        ext_scr[k, halo : halo + columns] = all_ref[base + k - 1]

    @pl.when(base == 0)
    def _():
        ext_scr[0, halo : halo + columns] = north_ref[0]

    @pl.when(base > 0)
    def _():
        ext_scr[0, halo : halo + columns] = all_ref[jnp.maximum(base - 1, 0)]

    @pl.when(base + rows == lat_rows)
    def _():
        ext_scr[rows + 1, halo : halo + columns] = south_ref[0]

    @pl.when(base + rows < lat_rows)
    def _():
        ext_scr[rows + 1, halo : halo + columns] = all_ref[jnp.minimum(base + rows, lat_rows - 1)]

    ext_scr[rows + 2] = jnp.zeros(ext_scr.shape[1:], ext_scr.dtype)
    def needed(q):
        inside = (base + q >= scalar_ref[0]) & (base + q < scalar_ref[0] + POLAR)
        return jnp.logical_not(inside & (scalar_ref[1] != 0))

    conv_block(ext_scr, src_ref, f_ref, w_ref, o_ref, conv_scr, 0, needed)


def wide_kernel(scalar_ref, ext_ref, src_ref, f_ref, w_ref, prev_ref, o_ref, conv_scr):
    @pl.when(scalar_ref[1] != 0)
    def _():
        conv_block(ext_ref, src_ref, f_ref, w_ref, o_ref, conv_scr, 0)

    @pl.when(scalar_ref[1] == 0)
    def _():
        o_ref[...] = prev_ref[...]


def full_spec(shape):
    return pl.BlockSpec(shape, lambda i, s: (0,) * len(shape))


def near_call(scalars, sources, features, west, east, north, south, mix_weight,
              first, count_rows, lowest, previous=None):
    lat_rows, columns, channels = features.shape
    count = mix_weight.shape[0]
    halo = NEAR
    offset = first // NEAR_BLOCK
    row_map = lambda i, s: (i + offset, 0, 0)
    in_specs = [
        pl.BlockSpec((NEAR_BLOCK,) + sources.shape[1:], row_map),
        pl.BlockSpec((NEAR_BLOCK, columns, channels), row_map),
        full_spec(features.shape), full_spec(west.shape), full_spec(east.shape),
        full_spec(north.shape), full_spec(south.shape), full_spec(mix_weight.shape),
    ]
    operands = [scalars, sources, features, features, west, east, north, south, mix_weight]
    aliases = {}
    if previous is not None:
        in_specs.append(pl.BlockSpec(memory_space=pl.ANY))
        operands.append(previous)
        aliases = {len(operands) - 1: 0}
    grid_spec = pltpu.PrefetchScalarGridSpec(
        num_scalar_prefetch=1,
        grid=(count_rows // NEAR_BLOCK,),
        in_specs=in_specs,
        out_specs=pl.BlockSpec((NEAR_BLOCK, columns, channels), row_map),
        scratch_shapes=[
            pltpu.VMEM((NEAR_BLOCK + 3, columns + 2 * halo, channels), features.dtype),
            pltpu.VMEM((count, NEAR_BLOCK * columns, channels), jnp.bfloat16),
        ],
    )
    return pl.pallas_call(
        functools.partial(near_kernel, first=first, lowest=lowest), grid_spec=grid_spec,
        out_shape=jax.ShapeDtypeStruct(features.shape, features.dtype),
        input_output_aliases=aliases,
    )(*operands)


def wide_call(scalars, extended, sources, features, mix_weight, previous):
    lat_rows, columns, channels = features.shape
    count = mix_weight.shape[0]
    row_map = lambda i, s: (s[0] // BLOCK + i, 0, 0)
    grid_spec = pltpu.PrefetchScalarGridSpec(
        num_scalar_prefetch=1,
        grid=(sources.shape[0] // BLOCK,),
        in_specs=[
            full_spec(extended.shape),
            pl.BlockSpec((BLOCK,) + sources.shape[1:], lambda i, s: (i, 0, 0)),
            pl.BlockSpec((BLOCK, columns, channels), row_map),
            full_spec(mix_weight.shape),
            pl.BlockSpec((BLOCK, columns, channels), row_map),
        ],
        out_specs=pl.BlockSpec((BLOCK, columns, channels), row_map),
        scratch_shapes=[pltpu.VMEM((count, BLOCK * columns, channels), jnp.bfloat16)],
    )
    return pl.pallas_call(
        wide_kernel, grid_spec=grid_spec,
        out_shape=jax.ShapeDtypeStruct(features.shape, features.dtype),
        input_output_aliases={5: 0},
    )(scalars, extended, sources, features, mix_weight, previous)


def body(features, quad_weights, cycle_index, widths, mix_weight):
    count = mix_weight.shape[0]
    lat_rows, columns, channels = features.shape
    reach = quad_weights.shape[2] // 2
    hops = reach // columns

    lat_index, lat_count = lax.axis_index("lat"), lax.axis_size("lat")
    last_band = lat_index == lat_count - 1
    polar = (lat_index == 0) | last_band
    start = jnp.where(last_band, lat_rows - POLAR, 0).astype(jnp.int32)
    scalars = jnp.stack([start, polar.astype(jnp.int32)])

    zero_row = jnp.zeros((1, columns, channels), features.dtype)
    window = lax.dynamic_slice_in_dim(
        jnp.concatenate([zero_row, features, zero_row], axis=0), start, POLAR + 2, 0)
    flat_window = window.reshape(-1, channels)
    count_lat = lax.axis_size("lat")
    up = [(i, i + 1) for i in range(count_lat - 1)]
    down = [(j, i) for i, j in up]
    north = lax.ppermute(features[lat_rows - 1 :], "lat", up)
    south = lax.ppermute(features[:1], "lat", down)
    padded = jnp.concatenate([north, features, south], axis=0)
    half = lat_rows // 2
    head = padded[: half + 2]
    tail = padded[half:]
    head_west = shifted(head[:, columns - NEAR :].reshape(-1, channels), "lon", 1)
    head_east = shifted(head[:, :NEAR].reshape(-1, channels), "lon", -1)
    from_west = shifted(jnp.concatenate(
        [tail[:, columns - NEAR :].reshape(-1, channels), flat_window]), "lon", 1)
    from_east = shifted(jnp.concatenate(
        [tail[:, :NEAR].reshape(-1, channels), flat_window]), "lon", -1)
    near_count = tail.shape[0] * NEAR
    west_far = [shifted(window, "lon", hop) for hop in range(hops, 1, -1)]
    east_far = [shifted(window, "lon", -hop) for hop in range(2, hops + 1)]

    basis_values = basis_table(quad_weights, cycle_index, widths, count)
    near_sources = flat_sources(
        basis_values[:, :, :, reach - NEAR : reach + NEAR + 1], columns + 2 * NEAR, 256)
    polar_values = lax.dynamic_slice_in_dim(basis_values, start, POLAR, 0)
    wide_sources = flat_sources(polar_values, columns + 2 * reach, 512)

    out = near_call(scalars, near_sources, features, head_west, head_east, north, south,
                    mix_weight, 0, half, -1)
    out = near_call(scalars, near_sources, features, from_west, from_east, north, south,
                    mix_weight, half, lat_rows - half, half - 1, previous=out)

    west_one = from_west[near_count:].reshape(window.shape)
    east_one = from_east[near_count:].reshape(window.shape)
    wide = jnp.concatenate(west_far + [west_one, window, east_one] + east_far, axis=1)
    wide = wide[:, hops * columns - reach : hops * columns + columns + reach]
    wide = jnp.pad(wide, ((0, 1), (0, 0), (0, 0)))
    return wide_call(scalars, wide, wide_sources, features, mix_weight, out)


def solution(mesh):
    in_specs = (P("lat", "lon", None), P("lat", None, None), P("lat", None, None), P("lat"), P())
    out_specs = P("lat", "lon", None)
    return jax.shard_map(body, mesh=mesh, in_specs=in_specs, out_specs=out_specs, check_vma=False)
```

```python
import functools

import jax
import jax.numpy as jnp
from jax import lax
from jax.experimental import pallas as pl
from jax.experimental.pallas import tpu as pltpu
from jax.sharding import PartitionSpec as P

POLAR = 8
NEAR = 16
BLOCK = 8
NEAR_BLOCK = 24


def shifted(block, axis, distance):
    devices = range(lax.axis_size(axis))
    route = [((i - distance) % len(devices), i) for i in devices]
    return lax.ppermute(block, axis, route)


def lat_extended(value):
    count, length = lax.axis_size("lat"), value.shape[0]
    up = [(i, i + 1) for i in range(count - 1)]
    down = [(j, i) for i, j in up]
    before = lax.ppermute(value[length - 1 :], "lat", up)
    after = lax.ppermute(value[:1], "lat", down)
    return jnp.concatenate([before, value, after], axis=0)


def basis_table(quad_weights, cycle_index, widths, count):
    offsets = jnp.arange(quad_weights.shape[2]) - quad_weights.shape[2] // 2
    inside = jnp.abs(offsets)[None, None, :] <= widths[:, None, None]
    member = cycle_index[:, None, :, :] == jnp.arange(count)[None, :, None, None]
    scale_row = 1.0 / jnp.sqrt(3.0 * (2.0 * widths.astype(jnp.float32) + 1.0))
    values = jnp.where(
        member & inside[:, None, :, :], quad_weights[:, None, :, :], jnp.float32(0.0)
    )
    return (values * scale_row[:, None, None, None]).astype(jnp.bfloat16)


def flat_sources(values, span, lanes):
    rows, count, offsets, taps = values.shape
    flat = jnp.pad(values, ((0, 0), (0, 0), (0, 0), (0, span - taps)))
    flat = flat.reshape(rows, count, offsets * span)
    return jnp.pad(flat, ((0, 0), (0, 0), (0, lanes - offsets * span)))


def conv_block(ext_ref, src_ref, f_ref, w_ref, o_ref, conv_scr, base, before_mix=None):
    rows, columns, channels = f_ref.shape
    count, lanes = src_ref.shape[1], src_ref.shape[2]
    span = ext_ref.shape[1]
    for q in range(rows):
        source = src_ref[q].astype(jnp.float32)
        pieces = []
        for b in range(count):
            spread = jnp.broadcast_to(source[b : b + 1], (columns, lanes))
            pieces.append(pltpu.roll(spread, 0, 1, stride=1, stride_axis=0))
        kernel = jnp.concatenate(pieces, axis=0).astype(jnp.bfloat16)
        window = ext_ref[pl.ds(base + q, 4)].reshape(4 * span, channels)[:lanes]
        conv = jnp.dot(kernel, window, preferred_element_type=jnp.float32)
        conv = conv.astype(jnp.bfloat16)
        for b in range(count):
            conv_scr[b, q * columns : (q + 1) * columns, :] = conv[b * columns : (b + 1) * columns]
    if before_mix is not None:
        before_mix()
    acc = f_ref[...].reshape(rows * columns, channels).astype(jnp.float32)
    for b in range(count):
        acc = acc + jnp.dot(conv_scr[b], w_ref[b], preferred_element_type=jnp.float32)
    o_ref[...] = acc.reshape(rows, columns, channels).astype(o_ref.dtype)


def near_kernel(scalar_ref, src_ref, f_ref, prev_ref, next_ref, west_ref, east_ref,
                north_ref, south_ref, w_hbm, *rest, first, lowest, lat_rows):
    o_ref, ext_scr, conv_scr, w_ref, w_sem = rest[-5:]
    rows, columns, channels = f_ref.shape
    halo = (ext_scr.shape[1] - columns) // 2
    step = pl.program_id(0)
    base = first + step * rows
    weights = pltpu.make_async_copy(w_hbm, w_ref, w_sem)

    @pl.when(step == 0)
    def _():
        weights.start()

    def sides(k, row):
        start = pl.multiple_of((row - lowest) * halo, halo)
        ext_scr[k, :halo] = west_ref[pl.ds(start, halo)]
        ext_scr[k, halo + columns :] = east_ref[pl.ds(start, halo)]

    for k in range(rows + 2):
        sides(k, base + k - 1)
    for k in range(1, rows + 1):
        ext_scr[k, halo : halo + columns] = f_ref[k - 1]

    @pl.when(base == 0)
    def _():
        ext_scr[0, halo : halo + columns] = north_ref[0]

    @pl.when(base > 0)
    def _():
        ext_scr[0, halo : halo + columns] = prev_ref[0]

    @pl.when(base + rows == lat_rows)
    def _():
        ext_scr[rows + 1, halo : halo + columns] = south_ref[0]

    @pl.when(base + rows < lat_rows)
    def _():
        ext_scr[rows + 1, halo : halo + columns] = next_ref[0]

    ext_scr[rows + 2] = jnp.zeros(ext_scr.shape[1:], ext_scr.dtype)

    def wait_weights():
        @pl.when(step == 0)
        def _():
            weights.wait()

    conv_block(ext_scr, src_ref, f_ref, w_ref, o_ref, conv_scr, 0, wait_weights)


def wide_kernel(scalar_ref, ext_ref, src_ref, f_ref, w_ref, prev_ref, o_ref, conv_scr):
    @pl.when(scalar_ref[1] != 0)
    def _():
        conv_block(ext_ref, src_ref, f_ref, w_ref, o_ref, conv_scr, 0)

    @pl.when(scalar_ref[1] == 0)
    def _():
        o_ref[...] = prev_ref[...]


def full_spec(shape):
    return pl.BlockSpec(shape, lambda i, s: (0,) * len(shape))


def near_call(scalars, sources, features, west, east, north, south, mix_weight,
              first, count_rows, lowest, previous=None):
    lat_rows, columns, channels = features.shape
    count = mix_weight.shape[0]
    halo = NEAR
    offset = first // NEAR_BLOCK
    row_map = lambda i, s: (i + offset, 0, 0)
    prev_map = lambda i, s: (jnp.maximum(first + i * NEAR_BLOCK - 1, 0), 0, 0)
    next_map = lambda i, s: (jnp.minimum(first + (i + 1) * NEAR_BLOCK, lat_rows - 1), 0, 0)
    in_specs = [
        pl.BlockSpec((NEAR_BLOCK,) + sources.shape[1:], row_map),
        pl.BlockSpec((NEAR_BLOCK, columns, channels), row_map),
        pl.BlockSpec((1, columns, channels), prev_map),
        pl.BlockSpec((1, columns, channels), next_map),
        full_spec(west.shape), full_spec(east.shape),
        full_spec(north.shape), full_spec(south.shape), pl.BlockSpec(memory_space=pl.ANY),
    ]
    operands = [scalars, sources, features, features, features, west, east, north, south,
                mix_weight]
    aliases = {}
    if previous is not None:
        in_specs.append(pl.BlockSpec(memory_space=pl.ANY))
        operands.append(previous)
        aliases = {len(operands) - 1: 0}
    grid_spec = pltpu.PrefetchScalarGridSpec(
        num_scalar_prefetch=1,
        grid=(count_rows // NEAR_BLOCK,),
        in_specs=in_specs,
        out_specs=pl.BlockSpec((NEAR_BLOCK, columns, channels), row_map),
        scratch_shapes=[
            pltpu.VMEM((NEAR_BLOCK + 3, columns + 2 * halo, channels), features.dtype),
            pltpu.VMEM((count, NEAR_BLOCK * columns, channels), jnp.bfloat16),
            pltpu.VMEM(mix_weight.shape, mix_weight.dtype),
            pltpu.SemaphoreType.DMA(()),
        ],
    )
    return pl.pallas_call(
        functools.partial(near_kernel, first=first, lowest=lowest, lat_rows=lat_rows),
        grid_spec=grid_spec,
        out_shape=jax.ShapeDtypeStruct(features.shape, features.dtype),
        input_output_aliases=aliases,
    )(*operands)


def wide_call(scalars, extended, sources, features, mix_weight, previous):
    lat_rows, columns, channels = features.shape
    count = mix_weight.shape[0]
    row_map = lambda i, s: (s[0] // BLOCK + i, 0, 0)
    grid_spec = pltpu.PrefetchScalarGridSpec(
        num_scalar_prefetch=1,
        grid=(sources.shape[0] // BLOCK,),
        in_specs=[
            full_spec(extended.shape),
            pl.BlockSpec((BLOCK,) + sources.shape[1:], lambda i, s: (i, 0, 0)),
            pl.BlockSpec((BLOCK, columns, channels), row_map),
            full_spec(mix_weight.shape),
            pl.BlockSpec((BLOCK, columns, channels), row_map),
        ],
        out_specs=pl.BlockSpec((BLOCK, columns, channels), row_map),
        scratch_shapes=[pltpu.VMEM((count, BLOCK * columns, channels), jnp.bfloat16)],
    )
    return pl.pallas_call(
        wide_kernel, grid_spec=grid_spec,
        out_shape=jax.ShapeDtypeStruct(features.shape, features.dtype),
        input_output_aliases={5: 0},
    )(scalars, extended, sources, features, mix_weight, previous)


def body(features, quad_weights, cycle_index, widths, mix_weight):
    count = mix_weight.shape[0]
    lat_rows, columns, channels = features.shape
    reach = quad_weights.shape[2] // 2
    hops = reach // columns

    lat_index, lat_count = lax.axis_index("lat"), lax.axis_size("lat")
    last_band = lat_index == lat_count - 1
    polar = (lat_index == 0) | last_band
    start = jnp.where(last_band, lat_rows - POLAR, 0).astype(jnp.int32)
    scalars = jnp.stack([start, polar.astype(jnp.int32)])

    zero_row = jnp.zeros((1, columns, channels), features.dtype)
    window = lax.dynamic_slice_in_dim(
        jnp.concatenate([zero_row, features, zero_row], axis=0), start, POLAR + 2, 0)
    flat_window = window.reshape(-1, channels)
    count_lat = lax.axis_size("lat")
    up = [(i, i + 1) for i in range(count_lat - 1)]
    down = [(j, i) for i, j in up]
    north = lax.ppermute(features[lat_rows - 1 :], "lat", up)
    south = lax.ppermute(features[:1], "lat", down)
    padded = jnp.concatenate([north, features, south], axis=0)
    half = lat_rows // 2
    head = padded[: half + 2]
    tail = padded[half:]
    head_west = shifted(head[:, columns - NEAR :].reshape(-1, channels), "lon", 1)
    head_east = shifted(head[:, :NEAR].reshape(-1, channels), "lon", -1)
    from_west = shifted(jnp.concatenate(
        [tail[:, columns - NEAR :].reshape(-1, channels), flat_window]), "lon", 1)
    from_east = shifted(jnp.concatenate(
        [tail[:, :NEAR].reshape(-1, channels), flat_window]), "lon", -1)
    near_count = tail.shape[0] * NEAR
    west_far = [shifted(window, "lon", hop) for hop in range(hops, 1, -1)]
    east_far = [shifted(window, "lon", -hop) for hop in range(2, hops + 1)]

    basis_values = basis_table(quad_weights, cycle_index, widths, count)
    near_sources = flat_sources(
        basis_values[:, :, :, reach - NEAR : reach + NEAR + 1], columns + 2 * NEAR, 256)
    polar_values = lax.dynamic_slice_in_dim(basis_values, start, POLAR, 0)
    wide_sources = flat_sources(polar_values, columns + 2 * reach, 512)

    out = near_call(scalars, near_sources, features, head_west, head_east, north, south,
                    mix_weight, 0, half, -1)
    out = near_call(scalars, near_sources, features, from_west, from_east, north, south,
                    mix_weight, half, lat_rows - half, half - 1, previous=out)

    west_one = from_west[near_count:].reshape(window.shape)
    east_one = from_east[near_count:].reshape(window.shape)
    wide = jnp.concatenate(west_far + [west_one, window, east_one] + east_far, axis=1)
    wide = wide[:, hops * columns - reach : hops * columns + columns + reach]
    wide = jnp.pad(wide, ((0, 1), (0, 0), (0, 0)))
    return wide_call(scalars, wide, wide_sources, features, mix_weight, out)


def solution(mesh):
    in_specs = (P("lat", "lon", None), P("lat", None, None), P("lat", None, None), P("lat"), P())
    out_specs = P("lat", "lon", None)
    return jax.shard_map(body, mesh=mesh, in_specs=in_specs, out_specs=out_specs, check_vma=False)
```

```python
import functools

import jax
import jax.numpy as jnp
from jax import lax
from jax.experimental import pallas as pl
from jax.experimental.pallas import tpu as pltpu
from jax.sharding import PartitionSpec as P

POLAR = 8
NEAR = 16
BLOCK = 8
NEAR_BLOCK = 24


def shifted(block, axis, distance):
    devices = range(lax.axis_size(axis))
    route = [((i - distance) % len(devices), i) for i in devices]
    return lax.ppermute(block, axis, route)


def lat_extended(value):
    count, length = lax.axis_size("lat"), value.shape[0]
    up = [(i, i + 1) for i in range(count - 1)]
    down = [(j, i) for i, j in up]
    before = lax.ppermute(value[length - 1 :], "lat", up)
    after = lax.ppermute(value[:1], "lat", down)
    return jnp.concatenate([before, value, after], axis=0)


def basis_table(quad_weights, cycle_index, widths, count):
    offsets = jnp.arange(quad_weights.shape[2]) - quad_weights.shape[2] // 2
    inside = jnp.abs(offsets)[None, None, :] <= widths[:, None, None]
    member = cycle_index[:, None, :, :] == jnp.arange(count)[None, :, None, None]
    scale_row = 1.0 / jnp.sqrt(3.0 * (2.0 * widths.astype(jnp.float32) + 1.0))
    values = jnp.where(
        member & inside[:, None, :, :], quad_weights[:, None, :, :], jnp.float32(0.0)
    )
    return (values * scale_row[:, None, None, None]).astype(jnp.bfloat16)


def flat_sources(values, span, lanes):
    rows, count, offsets, taps = values.shape
    flat = jnp.pad(values, ((0, 0), (0, 0), (0, 0), (0, span - taps)))
    flat = flat.reshape(rows, count, offsets * span)
    return jnp.pad(flat, ((0, 0), (0, 0), (0, lanes - offsets * span)))


def conv_block(ext_ref, src_ref, f_ref, w_ref, o_ref, conv_scr, base, before_mix=None):
    rows, columns, channels = f_ref.shape
    count, lanes = src_ref.shape[1], src_ref.shape[2]
    span = ext_ref.shape[1]
    for q in range(rows):
        source = src_ref[q].astype(jnp.float32)
        pieces = []
        for b in range(count):
            spread = jnp.broadcast_to(source[b : b + 1], (columns, lanes))
            pieces.append(pltpu.roll(spread, 0, 1, stride=1, stride_axis=0))
        kernel = jnp.concatenate(pieces, axis=0).astype(jnp.bfloat16)
        window = ext_ref[pl.ds(base + q, 4)].reshape(4 * span, channels)[:lanes]
        conv = jnp.dot(kernel, window, preferred_element_type=jnp.float32)
        conv = conv.astype(jnp.bfloat16)
        for b in range(count):
            conv_scr[b, q * columns : (q + 1) * columns, :] = conv[b * columns : (b + 1) * columns]
    if before_mix is not None:
        before_mix()
    acc = f_ref[...].reshape(rows * columns, channels).astype(jnp.float32)
    for b in range(count):
        acc = acc + jnp.dot(conv_scr[b], w_ref[b], preferred_element_type=jnp.float32)
    o_ref[...] = acc.reshape(rows, columns, channels).astype(o_ref.dtype)


def near_kernel(scalar_ref, src_ref, f_ref, prev_ref, next_ref, west_ref, east_ref,
                north_ref, south_ref, w_hbm, *rest, first, lowest, lat_rows):
    o_ref, ext_scr, conv_scr, w_ref, w_sem = rest[-5:]
    rows, columns, channels = f_ref.shape
    halo = (ext_scr.shape[1] - columns) // 2
    step = pl.program_id(0)
    base = first + step * rows
    weights = pltpu.make_async_copy(w_hbm, w_ref, w_sem)

    @pl.when(step == 0)
    def _():
        weights.start()

    def sides(k, row):
        start = pl.multiple_of((row - lowest) * halo, halo)
        ext_scr[k, :halo] = west_ref[pl.ds(start, halo)]
        ext_scr[k, halo + columns :] = east_ref[pl.ds(start, halo)]

    for k in range(rows + 2):
        sides(k, base + k - 1)
    for k in range(1, rows + 1):
        ext_scr[k, halo : halo + columns] = f_ref[k - 1]

    @pl.when(base == 0)
    def _():
        ext_scr[0, halo : halo + columns] = north_ref[0]

    @pl.when(base > 0)
    def _():
        ext_scr[0, halo : halo + columns] = prev_ref[0]

    @pl.when(base + rows == lat_rows)
    def _():
        ext_scr[rows + 1, halo : halo + columns] = south_ref[0]

    @pl.when(base + rows < lat_rows)
    def _():
        ext_scr[rows + 1, halo : halo + columns] = next_ref[0]

    ext_scr[rows + 2] = jnp.zeros(ext_scr.shape[1:], ext_scr.dtype)

    def wait_weights():
        @pl.when(step == 0)
        def _():
            weights.wait()

    conv_block(ext_scr, src_ref, f_ref, w_ref, o_ref, conv_scr, 0, wait_weights)


def wide_kernel(scalar_ref, ext_ref, src_ref, f_ref, w_hbm, prev_ref, o_ref, conv_scr, w_ref,
                w_sem):
    @pl.when(scalar_ref[1] != 0)
    def _():
        weights = pltpu.make_async_copy(w_hbm, w_ref, w_sem)
        weights.start()
        conv_block(ext_ref, src_ref, f_ref, w_ref, o_ref, conv_scr, 0, weights.wait)

    @pl.when(scalar_ref[1] == 0)
    def _():
        o_ref[...] = prev_ref[...]


def full_spec(shape):
    return pl.BlockSpec(shape, lambda i, s: (0,) * len(shape))


def near_call(scalars, sources, features, west, east, north, south, mix_weight,
              first, count_rows, lowest, previous=None):
    lat_rows, columns, channels = features.shape
    count = mix_weight.shape[0]
    halo = NEAR
    offset = first // NEAR_BLOCK
    row_map = lambda i, s: (i + offset, 0, 0)
    prev_map = lambda i, s: (jnp.maximum(first + i * NEAR_BLOCK - 1, 0), 0, 0)
    next_map = lambda i, s: (jnp.minimum(first + (i + 1) * NEAR_BLOCK, lat_rows - 1), 0, 0)
    in_specs = [
        pl.BlockSpec((NEAR_BLOCK,) + sources.shape[1:], row_map),
        pl.BlockSpec((NEAR_BLOCK, columns, channels), row_map),
        pl.BlockSpec((1, columns, channels), prev_map),
        pl.BlockSpec((1, columns, channels), next_map),
        full_spec(west.shape), full_spec(east.shape),
        full_spec(north.shape), full_spec(south.shape), pl.BlockSpec(memory_space=pl.ANY),
    ]
    operands = [scalars, sources, features, features, features, west, east, north, south,
                mix_weight]
    aliases = {}
    if previous is not None:
        in_specs.append(pl.BlockSpec(memory_space=pl.ANY))
        operands.append(previous)
        aliases = {len(operands) - 1: 0}
    grid_spec = pltpu.PrefetchScalarGridSpec(
        num_scalar_prefetch=1,
        grid=(count_rows // NEAR_BLOCK,),
        in_specs=in_specs,
        out_specs=pl.BlockSpec((NEAR_BLOCK, columns, channels), row_map),
        scratch_shapes=[
            pltpu.VMEM((NEAR_BLOCK + 3, columns + 2 * halo, channels), features.dtype),
            pltpu.VMEM((count, NEAR_BLOCK * columns, channels), jnp.bfloat16),
            pltpu.VMEM(mix_weight.shape, mix_weight.dtype),
            pltpu.SemaphoreType.DMA(()),
        ],
    )
    return pl.pallas_call(
        functools.partial(near_kernel, first=first, lowest=lowest, lat_rows=lat_rows),
        grid_spec=grid_spec,
        out_shape=jax.ShapeDtypeStruct(features.shape, features.dtype),
        input_output_aliases=aliases,
    )(*operands)


def wide_call(scalars, extended, sources, features, mix_weight, previous):
    lat_rows, columns, channels = features.shape
    count = mix_weight.shape[0]
    row_map = lambda i, s: (s[0] // BLOCK + i, 0, 0)
    grid_spec = pltpu.PrefetchScalarGridSpec(
        num_scalar_prefetch=1,
        grid=(sources.shape[0] // BLOCK,),
        in_specs=[
            full_spec(extended.shape),
            pl.BlockSpec((BLOCK,) + sources.shape[1:], lambda i, s: (i, 0, 0)),
            pl.BlockSpec((BLOCK, columns, channels), row_map),
            pl.BlockSpec(memory_space=pl.ANY),
            pl.BlockSpec((BLOCK, columns, channels), row_map),
        ],
        out_specs=pl.BlockSpec((BLOCK, columns, channels), row_map),
        scratch_shapes=[
            pltpu.VMEM((count, BLOCK * columns, channels), jnp.bfloat16),
            pltpu.VMEM(mix_weight.shape, mix_weight.dtype),
            pltpu.SemaphoreType.DMA(()),
        ],
    )
    return pl.pallas_call(
        wide_kernel, grid_spec=grid_spec,
        out_shape=jax.ShapeDtypeStruct(features.shape, features.dtype),
        input_output_aliases={5: 0},
    )(scalars, extended, sources, features, mix_weight, previous)


def body(features, quad_weights, cycle_index, widths, mix_weight):
    count = mix_weight.shape[0]
    lat_rows, columns, channels = features.shape
    reach = quad_weights.shape[2] // 2
    hops = reach // columns

    lat_index, lat_count = lax.axis_index("lat"), lax.axis_size("lat")
    last_band = lat_index == lat_count - 1
    polar = (lat_index == 0) | last_band
    start = jnp.where(last_band, lat_rows - POLAR, 0).astype(jnp.int32)
    scalars = jnp.stack([start, polar.astype(jnp.int32)])

    zero_row = jnp.zeros((1, columns, channels), features.dtype)
    window = lax.dynamic_slice_in_dim(
        jnp.concatenate([zero_row, features, zero_row], axis=0), start, POLAR + 2, 0)
    flat_window = window.reshape(-1, channels)
    count_lat = lax.axis_size("lat")
    up = [(i, i + 1) for i in range(count_lat - 1)]
    down = [(j, i) for i, j in up]
    north = lax.ppermute(features[lat_rows - 1 :], "lat", up)
    south = lax.ppermute(features[:1], "lat", down)
    padded = jnp.concatenate([north, features, south], axis=0)
    half = lat_rows // 2
    head = padded[: half + 2]
    tail = padded[half:]
    head_west = shifted(head[:, columns - NEAR :].reshape(-1, channels), "lon", 1)
    head_east = shifted(head[:, :NEAR].reshape(-1, channels), "lon", -1)
    from_west = shifted(jnp.concatenate(
        [tail[:, columns - NEAR :].reshape(-1, channels), flat_window]), "lon", 1)
    from_east = shifted(jnp.concatenate(
        [tail[:, :NEAR].reshape(-1, channels), flat_window]), "lon", -1)
    near_count = tail.shape[0] * NEAR
    west_far = [shifted(window, "lon", hop) for hop in range(hops, 1, -1)]
    east_far = [shifted(window, "lon", -hop) for hop in range(2, hops + 1)]

    basis_values = basis_table(quad_weights, cycle_index, widths, count)
    near_sources = flat_sources(
        basis_values[:, :, :, reach - NEAR : reach + NEAR + 1], columns + 2 * NEAR, 256)
    polar_values = lax.dynamic_slice_in_dim(basis_values, start, POLAR, 0)
    wide_sources = flat_sources(polar_values, columns + 2 * reach, 512)

    out = near_call(scalars, near_sources, features, head_west, head_east, north, south,
                    mix_weight, 0, half, -1)
    out = near_call(scalars, near_sources, features, from_west, from_east, north, south,
                    mix_weight, half, lat_rows - half, half - 1, previous=out)

    west_one = from_west[near_count:].reshape(window.shape)
    east_one = from_east[near_count:].reshape(window.shape)
    wide = jnp.concatenate(west_far + [west_one, window, east_one] + east_far, axis=1)
    wide = wide[:, hops * columns - reach : hops * columns + columns + reach]
    wide = jnp.pad(wide, ((0, 1), (0, 0), (0, 0)))
    return wide_call(scalars, wide, wide_sources, features, mix_weight, out)


def solution(mesh):
    in_specs = (P("lat", "lon", None), P("lat", None, None), P("lat", None, None), P("lat"), P())
    out_specs = P("lat", "lon", None)
    return jax.shard_map(body, mesh=mesh, in_specs=in_specs, out_specs=out_specs, check_vma=False)
```

```python
import functools

import jax
import jax.numpy as jnp
from jax import lax
from jax.experimental import pallas as pl
from jax.experimental.pallas import tpu as pltpu
from jax.sharding import PartitionSpec as P

POLAR = 8
NEAR = 16
BLOCK = 8
NEAR_BLOCK = 48


def shifted(block, axis, distance):
    devices = range(lax.axis_size(axis))
    route = [((i - distance) % len(devices), i) for i in devices]
    return lax.ppermute(block, axis, route)


def lat_extended(value):
    count, length = lax.axis_size("lat"), value.shape[0]
    up = [(i, i + 1) for i in range(count - 1)]
    down = [(j, i) for i, j in up]
    before = lax.ppermute(value[length - 1 :], "lat", up)
    after = lax.ppermute(value[:1], "lat", down)
    return jnp.concatenate([before, value, after], axis=0)


def basis_table(quad_weights, cycle_index, widths, count):
    offsets = jnp.arange(quad_weights.shape[2]) - quad_weights.shape[2] // 2
    inside = jnp.abs(offsets)[None, None, :] <= widths[:, None, None]
    member = cycle_index[:, None, :, :] == jnp.arange(count)[None, :, None, None]
    scale_row = 1.0 / jnp.sqrt(3.0 * (2.0 * widths.astype(jnp.float32) + 1.0))
    values = jnp.where(
        member & inside[:, None, :, :], quad_weights[:, None, :, :], jnp.float32(0.0)
    )
    return (values * scale_row[:, None, None, None]).astype(jnp.bfloat16)


def flat_sources(values, span, lanes):
    rows, count, offsets, taps = values.shape
    flat = jnp.pad(values, ((0, 0), (0, 0), (0, 0), (0, span - taps)))
    flat = flat.reshape(rows, count, offsets * span)
    return jnp.pad(flat, ((0, 0), (0, 0), (0, lanes - offsets * span)))


def conv_block(ext_ref, src_ref, f_ref, w_ref, o_ref, conv_scr, base, before_mix=None):
    rows, columns, channels = f_ref.shape
    count, lanes = src_ref.shape[1], src_ref.shape[2]
    span = ext_ref.shape[1]
    for q in range(rows):
        source = src_ref[q].astype(jnp.float32)
        pieces = []
        for b in range(count):
            spread = jnp.broadcast_to(source[b : b + 1], (columns, lanes))
            pieces.append(pltpu.roll(spread, 0, 1, stride=1, stride_axis=0))
        kernel = jnp.concatenate(pieces, axis=0).astype(jnp.bfloat16)
        window = ext_ref[pl.ds(base + q, 4)].reshape(4 * span, channels)[:lanes]
        conv = jnp.dot(kernel, window, preferred_element_type=jnp.float32)
        conv = conv.astype(jnp.bfloat16)
        for b in range(count):
            conv_scr[b, q * columns : (q + 1) * columns, :] = conv[b * columns : (b + 1) * columns]
    if before_mix is not None:
        before_mix()
    acc = f_ref[...].reshape(rows * columns, channels).astype(jnp.float32)
    for b in range(count):
        acc = acc + jnp.dot(conv_scr[b], w_ref[b], preferred_element_type=jnp.float32)
    o_ref[...] = acc.reshape(rows, columns, channels).astype(o_ref.dtype)


def near_kernel(scalar_ref, src_ref, f_ref, prev_ref, next_ref, west_ref, east_ref,
                north_ref, south_ref, w_hbm, *rest, first, lowest, lat_rows):
    o_ref, ext_scr, conv_scr, w_ref, w_sem = rest[-5:]
    rows, columns, channels = f_ref.shape
    halo = (ext_scr.shape[1] - columns) // 2
    step = pl.program_id(0)
    base = first + step * rows
    weights = pltpu.make_async_copy(w_hbm, w_ref, w_sem)

    @pl.when(step == 0)
    def _():
        weights.start()

    def sides(k, row):
        start = pl.multiple_of((row - lowest) * halo, halo)
        ext_scr[k, :halo] = west_ref[pl.ds(start, halo)]
        ext_scr[k, halo + columns :] = east_ref[pl.ds(start, halo)]

    for k in range(rows + 2):
        sides(k, base + k - 1)
    for k in range(1, rows + 1):
        ext_scr[k, halo : halo + columns] = f_ref[k - 1]

    @pl.when(base == 0)
    def _():
        ext_scr[0, halo : halo + columns] = north_ref[0]

    @pl.when(base > 0)
    def _():
        ext_scr[0, halo : halo + columns] = prev_ref[0]

    @pl.when(base + rows == lat_rows)
    def _():
        ext_scr[rows + 1, halo : halo + columns] = south_ref[0]

    @pl.when(base + rows < lat_rows)
    def _():
        ext_scr[rows + 1, halo : halo + columns] = next_ref[0]

    ext_scr[rows + 2] = jnp.zeros(ext_scr.shape[1:], ext_scr.dtype)

    def wait_weights():
        @pl.when(step == 0)
        def _():
            weights.wait()

    conv_block(ext_scr, src_ref, f_ref, w_ref, o_ref, conv_scr, 0, wait_weights)


def wide_kernel(scalar_ref, ext_ref, src_ref, f_ref, w_ref, prev_ref, o_ref, conv_scr):
    @pl.when(scalar_ref[1] != 0)
    def _():
        conv_block(ext_ref, src_ref, f_ref, w_ref, o_ref, conv_scr, 0)

    @pl.when(scalar_ref[1] == 0)
    def _():
        o_ref[...] = prev_ref[...]


def full_spec(shape):
    return pl.BlockSpec(shape, lambda i, s: (0,) * len(shape))


def near_call(scalars, sources, features, west, east, north, south, mix_weight,
              first, count_rows, lowest, previous=None):
    lat_rows, columns, channels = features.shape
    count = mix_weight.shape[0]
    halo = NEAR
    offset = first // NEAR_BLOCK
    row_map = lambda i, s: (i + offset, 0, 0)
    prev_map = lambda i, s: (jnp.maximum(first + i * NEAR_BLOCK - 1, 0), 0, 0)
    next_map = lambda i, s: (jnp.minimum(first + (i + 1) * NEAR_BLOCK, lat_rows - 1), 0, 0)
    in_specs = [
        pl.BlockSpec((NEAR_BLOCK,) + sources.shape[1:], row_map),
        pl.BlockSpec((NEAR_BLOCK, columns, channels), row_map),
        pl.BlockSpec((1, columns, channels), prev_map),
        pl.BlockSpec((1, columns, channels), next_map),
        full_spec(west.shape), full_spec(east.shape),
        full_spec(north.shape), full_spec(south.shape), pl.BlockSpec(memory_space=pl.ANY),
    ]
    operands = [scalars, sources, features, features, features, west, east, north, south,
                mix_weight]
    aliases = {}
    if previous is not None:
        in_specs.append(pl.BlockSpec(memory_space=pl.ANY))
        operands.append(previous)
        aliases = {len(operands) - 1: 0}
    grid_spec = pltpu.PrefetchScalarGridSpec(
        num_scalar_prefetch=1,
        grid=(count_rows // NEAR_BLOCK,),
        in_specs=in_specs,
        out_specs=pl.BlockSpec((NEAR_BLOCK, columns, channels), row_map),
        scratch_shapes=[
            pltpu.VMEM((NEAR_BLOCK + 3, columns + 2 * halo, channels), features.dtype),
            pltpu.VMEM((count, NEAR_BLOCK * columns, channels), jnp.bfloat16),
            pltpu.VMEM(mix_weight.shape, mix_weight.dtype),
            pltpu.SemaphoreType.DMA(()),
        ],
    )
    return pl.pallas_call(
        functools.partial(near_kernel, first=first, lowest=lowest, lat_rows=lat_rows),
        grid_spec=grid_spec,
        out_shape=jax.ShapeDtypeStruct(features.shape, features.dtype),
        input_output_aliases=aliases,
    )(*operands)


def wide_call(scalars, extended, sources, features, mix_weight, previous):
    lat_rows, columns, channels = features.shape
    count = mix_weight.shape[0]
    row_map = lambda i, s: (s[0] // BLOCK + i, 0, 0)
    grid_spec = pltpu.PrefetchScalarGridSpec(
        num_scalar_prefetch=1,
        grid=(sources.shape[0] // BLOCK,),
        in_specs=[
            full_spec(extended.shape),
            pl.BlockSpec((BLOCK,) + sources.shape[1:], lambda i, s: (i, 0, 0)),
            pl.BlockSpec((BLOCK, columns, channels), row_map),
            full_spec(mix_weight.shape),
            pl.BlockSpec((BLOCK, columns, channels), row_map),
        ],
        out_specs=pl.BlockSpec((BLOCK, columns, channels), row_map),
        scratch_shapes=[pltpu.VMEM((count, BLOCK * columns, channels), jnp.bfloat16)],
    )
    return pl.pallas_call(
        wide_kernel, grid_spec=grid_spec,
        out_shape=jax.ShapeDtypeStruct(features.shape, features.dtype),
        input_output_aliases={5: 0},
    )(scalars, extended, sources, features, mix_weight, previous)


def body(features, quad_weights, cycle_index, widths, mix_weight):
    count = mix_weight.shape[0]
    lat_rows, columns, channels = features.shape
    reach = quad_weights.shape[2] // 2
    hops = reach // columns

    lat_index, lat_count = lax.axis_index("lat"), lax.axis_size("lat")
    last_band = lat_index == lat_count - 1
    polar = (lat_index == 0) | last_band
    start = jnp.where(last_band, lat_rows - POLAR, 0).astype(jnp.int32)
    scalars = jnp.stack([start, polar.astype(jnp.int32)])

    zero_row = jnp.zeros((1, columns, channels), features.dtype)
    window = lax.dynamic_slice_in_dim(
        jnp.concatenate([zero_row, features, zero_row], axis=0), start, POLAR + 2, 0)
    flat_window = window.reshape(-1, channels)
    count_lat = lax.axis_size("lat")
    up = [(i, i + 1) for i in range(count_lat - 1)]
    down = [(j, i) for i, j in up]
    north = lax.ppermute(features[lat_rows - 1 :], "lat", up)
    south = lax.ppermute(features[:1], "lat", down)
    padded = jnp.concatenate([north, features, south], axis=0)
    half = lat_rows // 2
    head = padded[: half + 2]
    tail = padded[half:]
    head_west = shifted(head[:, columns - NEAR :].reshape(-1, channels), "lon", 1)
    head_east = shifted(head[:, :NEAR].reshape(-1, channels), "lon", -1)
    from_west = shifted(jnp.concatenate(
        [tail[:, columns - NEAR :].reshape(-1, channels), flat_window]), "lon", 1)
    from_east = shifted(jnp.concatenate(
        [tail[:, :NEAR].reshape(-1, channels), flat_window]), "lon", -1)
    near_count = tail.shape[0] * NEAR
    west_far = [shifted(window, "lon", hop) for hop in range(hops, 1, -1)]
    east_far = [shifted(window, "lon", -hop) for hop in range(2, hops + 1)]

    basis_values = basis_table(quad_weights, cycle_index, widths, count)
    near_sources = flat_sources(
        basis_values[:, :, :, reach - NEAR : reach + NEAR + 1], columns + 2 * NEAR, 256)
    polar_values = lax.dynamic_slice_in_dim(basis_values, start, POLAR, 0)
    wide_sources = flat_sources(polar_values, columns + 2 * reach, 512)

    out = near_call(scalars, near_sources, features, head_west, head_east, north, south,
                    mix_weight, 0, half, -1)
    out = near_call(scalars, near_sources, features, from_west, from_east, north, south,
                    mix_weight, half, lat_rows - half, half - 1, previous=out)

    west_one = from_west[near_count:].reshape(window.shape)
    east_one = from_east[near_count:].reshape(window.shape)
    wide = jnp.concatenate(west_far + [west_one, window, east_one] + east_far, axis=1)
    wide = wide[:, hops * columns - reach : hops * columns + columns + reach]
    wide = jnp.pad(wide, ((0, 1), (0, 0), (0, 0)))
    return wide_call(scalars, wide, wide_sources, features, mix_weight, out)


def solution(mesh):
    in_specs = (P("lat", "lon", None), P("lat", None, None), P("lat", None, None), P("lat"), P())
    out_specs = P("lat", "lon", None)
    return jax.shard_map(body, mesh=mesh, in_specs=in_specs, out_specs=out_specs, check_vma=False)
```

```python
import functools

import jax
import jax.numpy as jnp
from jax import lax
from jax.experimental import pallas as pl
from jax.experimental.pallas import tpu as pltpu
from jax.sharding import PartitionSpec as P

POLAR = 8
NEAR = 16
BLOCK = 8
NEAR_BLOCK = 32


def shifted(block, axis, distance):
    devices = range(lax.axis_size(axis))
    route = [((i - distance) % len(devices), i) for i in devices]
    return lax.ppermute(block, axis, route)


def lat_extended(value):
    count, length = lax.axis_size("lat"), value.shape[0]
    up = [(i, i + 1) for i in range(count - 1)]
    down = [(j, i) for i, j in up]
    before = lax.ppermute(value[length - 1 :], "lat", up)
    after = lax.ppermute(value[:1], "lat", down)
    return jnp.concatenate([before, value, after], axis=0)


def basis_table(quad_weights, cycle_index, widths, count):
    offsets = jnp.arange(quad_weights.shape[2]) - quad_weights.shape[2] // 2
    inside = jnp.abs(offsets)[None, None, :] <= widths[:, None, None]
    member = cycle_index[:, None, :, :] == jnp.arange(count)[None, :, None, None]
    scale_row = 1.0 / jnp.sqrt(3.0 * (2.0 * widths.astype(jnp.float32) + 1.0))
    values = jnp.where(
        member & inside[:, None, :, :], quad_weights[:, None, :, :], jnp.float32(0.0)
    )
    return (values * scale_row[:, None, None, None]).astype(jnp.bfloat16)


def flat_sources(values, span, lanes):
    rows, count, offsets, taps = values.shape
    flat = jnp.pad(values, ((0, 0), (0, 0), (0, 0), (0, span - taps)))
    flat = flat.reshape(rows, count, offsets * span)
    return jnp.pad(flat, ((0, 0), (0, 0), (0, lanes - offsets * span)))


def conv_block(ext_ref, src_ref, f_ref, w_ref, o_ref, conv_scr, base, before_mix=None):
    rows, columns, channels = f_ref.shape
    count, lanes = src_ref.shape[1], src_ref.shape[2]
    span = ext_ref.shape[1]
    for q in range(rows):
        source = src_ref[q].astype(jnp.float32)
        pieces = []
        for b in range(count):
            spread = jnp.broadcast_to(source[b : b + 1], (columns, lanes))
            pieces.append(pltpu.roll(spread, 0, 1, stride=1, stride_axis=0))
        kernel = jnp.concatenate(pieces, axis=0).astype(jnp.bfloat16)
        window = ext_ref[pl.ds(base + q, 4)].reshape(4 * span, channels)[:lanes]
        conv = jnp.dot(kernel, window, preferred_element_type=jnp.float32)
        conv = conv.astype(jnp.bfloat16)
        for b in range(count):
            conv_scr[b, q * columns : (q + 1) * columns, :] = conv[b * columns : (b + 1) * columns]
    if before_mix is not None:
        before_mix()
    acc = f_ref[...].reshape(rows * columns, channels).astype(jnp.float32)
    for b in range(count):
        acc = acc + jnp.dot(conv_scr[b], w_ref[b], preferred_element_type=jnp.float32)
    o_ref[...] = acc.reshape(rows, columns, channels).astype(o_ref.dtype)


def near_kernel(scalar_ref, src_ref, f_ref, prev_ref, next_ref, west_ref, east_ref,
                north_ref, south_ref, w_hbm, *rest, first, lowest, lat_rows):
    o_ref, ext_scr, conv_scr, w_ref, w_sem = rest[-5:]
    rows, columns, channels = f_ref.shape
    halo = (ext_scr.shape[1] - columns) // 2
    step = pl.program_id(0)
    base = first + step * rows
    weights = pltpu.make_async_copy(w_hbm, w_ref, w_sem)

    @pl.when(step == 0)
    def _():
        weights.start()

    def sides(k, row):
        start = pl.multiple_of((row - lowest) * halo, halo)
        ext_scr[k, :halo] = west_ref[pl.ds(start, halo)]
        ext_scr[k, halo + columns :] = east_ref[pl.ds(start, halo)]

    for k in range(rows + 2):
        sides(k, base + k - 1)
    for k in range(1, rows + 1):
        ext_scr[k, halo : halo + columns] = f_ref[k - 1]

    @pl.when(base == 0)
    def _():
        ext_scr[0, halo : halo + columns] = north_ref[0]

    @pl.when(base > 0)
    def _():
        ext_scr[0, halo : halo + columns] = prev_ref[0]

    @pl.when(base + rows == lat_rows)
    def _():
        ext_scr[rows + 1, halo : halo + columns] = south_ref[0]

    @pl.when(base + rows < lat_rows)
    def _():
        ext_scr[rows + 1, halo : halo + columns] = next_ref[0]

    ext_scr[rows + 2] = jnp.zeros(ext_scr.shape[1:], ext_scr.dtype)

    def wait_weights():
        @pl.when(step == 0)
        def _():
            weights.wait()

    conv_block(ext_scr, src_ref, f_ref, w_ref, o_ref, conv_scr, 0, wait_weights)


def wide_kernel(scalar_ref, ext_ref, src_ref, f_ref, w_ref, prev_ref, o_ref, conv_scr):
    @pl.when(scalar_ref[1] != 0)
    def _():
        conv_block(ext_ref, src_ref, f_ref, w_ref, o_ref, conv_scr, 0)

    @pl.when(scalar_ref[1] == 0)
    def _():
        o_ref[...] = prev_ref[...]


def full_spec(shape):
    return pl.BlockSpec(shape, lambda i, s: (0,) * len(shape))


def near_call(scalars, sources, features, west, east, north, south, mix_weight,
              first, count_rows, lowest, previous=None):
    lat_rows, columns, channels = features.shape
    count = mix_weight.shape[0]
    halo = NEAR
    offset = first // NEAR_BLOCK
    row_map = lambda i, s: (i + offset, 0, 0)
    prev_map = lambda i, s: (jnp.maximum(first + i * NEAR_BLOCK - 1, 0), 0, 0)
    next_map = lambda i, s: (jnp.minimum(first + (i + 1) * NEAR_BLOCK, lat_rows - 1), 0, 0)
    in_specs = [
        pl.BlockSpec((NEAR_BLOCK,) + sources.shape[1:], row_map),
        pl.BlockSpec((NEAR_BLOCK, columns, channels), row_map),
        pl.BlockSpec((1, columns, channels), prev_map),
        pl.BlockSpec((1, columns, channels), next_map),
        full_spec(west.shape), full_spec(east.shape),
        full_spec(north.shape), full_spec(south.shape), pl.BlockSpec(memory_space=pl.ANY),
    ]
    operands = [scalars, sources, features, features, features, west, east, north, south,
                mix_weight]
    aliases = {}
    if previous is not None:
        in_specs.append(pl.BlockSpec(memory_space=pl.ANY))
        operands.append(previous)
        aliases = {len(operands) - 1: 0}
    grid_spec = pltpu.PrefetchScalarGridSpec(
        num_scalar_prefetch=1,
        grid=(count_rows // NEAR_BLOCK,),
        in_specs=in_specs,
        out_specs=pl.BlockSpec((NEAR_BLOCK, columns, channels), row_map),
        scratch_shapes=[
            pltpu.VMEM((NEAR_BLOCK + 3, columns + 2 * halo, channels), features.dtype),
            pltpu.VMEM((count, NEAR_BLOCK * columns, channels), jnp.bfloat16),
            pltpu.VMEM(mix_weight.shape, mix_weight.dtype),
            pltpu.SemaphoreType.DMA(()),
        ],
    )
    return pl.pallas_call(
        functools.partial(near_kernel, first=first, lowest=lowest, lat_rows=lat_rows),
        grid_spec=grid_spec,
        out_shape=jax.ShapeDtypeStruct(features.shape, features.dtype),
        input_output_aliases=aliases,
    )(*operands)


def wide_call(scalars, extended, sources, features, mix_weight, previous):
    lat_rows, columns, channels = features.shape
    count = mix_weight.shape[0]
    row_map = lambda i, s: (s[0] // BLOCK + i, 0, 0)
    grid_spec = pltpu.PrefetchScalarGridSpec(
        num_scalar_prefetch=1,
        grid=(sources.shape[0] // BLOCK,),
        in_specs=[
            full_spec(extended.shape),
            pl.BlockSpec((BLOCK,) + sources.shape[1:], lambda i, s: (i, 0, 0)),
            pl.BlockSpec((BLOCK, columns, channels), row_map),
            full_spec(mix_weight.shape),
            pl.BlockSpec((BLOCK, columns, channels), row_map),
        ],
        out_specs=pl.BlockSpec((BLOCK, columns, channels), row_map),
        scratch_shapes=[pltpu.VMEM((count, BLOCK * columns, channels), jnp.bfloat16)],
    )
    return pl.pallas_call(
        wide_kernel, grid_spec=grid_spec,
        out_shape=jax.ShapeDtypeStruct(features.shape, features.dtype),
        input_output_aliases={5: 0},
    )(scalars, extended, sources, features, mix_weight, previous)


def body(features, quad_weights, cycle_index, widths, mix_weight):
    count = mix_weight.shape[0]
    lat_rows, columns, channels = features.shape
    reach = quad_weights.shape[2] // 2
    hops = reach // columns

    lat_index, lat_count = lax.axis_index("lat"), lax.axis_size("lat")
    last_band = lat_index == lat_count - 1
    polar = (lat_index == 0) | last_band
    start = jnp.where(last_band, lat_rows - POLAR, 0).astype(jnp.int32)
    scalars = jnp.stack([start, polar.astype(jnp.int32)])

    zero_row = jnp.zeros((1, columns, channels), features.dtype)
    window = lax.dynamic_slice_in_dim(
        jnp.concatenate([zero_row, features, zero_row], axis=0), start, POLAR + 2, 0)
    flat_window = window.reshape(-1, channels)
    count_lat = lax.axis_size("lat")
    up = [(i, i + 1) for i in range(count_lat - 1)]
    down = [(j, i) for i, j in up]
    north = lax.ppermute(features[lat_rows - 1 :], "lat", up)
    south = lax.ppermute(features[:1], "lat", down)
    padded = jnp.concatenate([north, features, south], axis=0)
    half = lat_rows // 3
    head = padded[: half + 2]
    tail = padded[half:]
    head_west = shifted(head[:, columns - NEAR :].reshape(-1, channels), "lon", 1)
    head_east = shifted(head[:, :NEAR].reshape(-1, channels), "lon", -1)
    from_west = shifted(jnp.concatenate(
        [tail[:, columns - NEAR :].reshape(-1, channels), flat_window]), "lon", 1)
    from_east = shifted(jnp.concatenate(
        [tail[:, :NEAR].reshape(-1, channels), flat_window]), "lon", -1)
    near_count = tail.shape[0] * NEAR
    west_far = [shifted(window, "lon", hop) for hop in range(hops, 1, -1)]
    east_far = [shifted(window, "lon", -hop) for hop in range(2, hops + 1)]

    basis_values = basis_table(quad_weights, cycle_index, widths, count)
    near_sources = flat_sources(
        basis_values[:, :, :, reach - NEAR : reach + NEAR + 1], columns + 2 * NEAR, 256)
    polar_values = lax.dynamic_slice_in_dim(basis_values, start, POLAR, 0)
    wide_sources = flat_sources(polar_values, columns + 2 * reach, 512)

    out = near_call(scalars, near_sources, features, head_west, head_east, north, south,
                    mix_weight, 0, half, -1)
    out = near_call(scalars, near_sources, features, from_west, from_east, north, south,
                    mix_weight, half, lat_rows - half, half - 1, previous=out)

    west_one = from_west[near_count:].reshape(window.shape)
    east_one = from_east[near_count:].reshape(window.shape)
    wide = jnp.concatenate(west_far + [west_one, window, east_one] + east_far, axis=1)
    wide = wide[:, hops * columns - reach : hops * columns + columns + reach]
    wide = jnp.pad(wide, ((0, 1), (0, 0), (0, 0)))
    return wide_call(scalars, wide, wide_sources, features, mix_weight, out)


def solution(mesh):
    in_specs = (P("lat", "lon", None), P("lat", None, None), P("lat", None, None), P("lat"), P())
    out_specs = P("lat", "lon", None)
    return jax.shard_map(body, mesh=mesh, in_specs=in_specs, out_specs=out_specs, check_vma=False)
```
